512 devices in a mesh: group: 32 (over z, core), vocab: 16 (over y, x).
Axes of the slice: x: 4, y: 4, z: 16, core: 2. Of those that a mesh axis runs over, the one named last changes fastest.
Arguments:
- hidden_in: bfloat16 [2, 2048, 2048], P(None, 'group'), may hold values from -6 to 6
- qkv_weight: bfloat16 [2, 2048, 6144], P(None, 'group', 'vocab'), may hold values from -0.125 to 0.125
- out_weight: bfloat16 [2, 2048, 2048], P(None, 'vocab', 'group'), may hold values from -0.125 to 0.125
- q_gain: float32 [2, 2048], P(None, 'vocab'), may hold values from 0.1 to 1.9
- k_gain: float32 [2, 2048], P(None, 'vocab'), may hold values from 0.1 to 1.9
- post_gain: float32 [2, 2048], replicated, may hold values from 0.1 to 1.9
- final_gain: float32 [2, 2048], replicated, may hold values from 0.1 to 1.9
- head_weight: bfloat16 [2, 2048, 100352], P(None, None, ('group', 'vocab'))
- pool_keys: bfloat16 [2, 2048, 16, 2048], P(None, 'group', None, 'vocab'), may hold values from -160 to 160
- pool_values: bfloat16 [2, 2048, 16, 2048], P(None, 'group', None, 'vocab'), may hold values from -6 to 6
- page_table: int32 [64, 32], replicated, may hold values from 0 to 2047, as said below
- deal: int32 [64], replicated, may hold values from 0 to 63, each once
- prompt_len: int32 [64], replicated, may hold values from 1 to 512, 13107 in all
- segment_ids: int32 [32, 64], replicated, may hold values from 0 to 1, never falling along the last dimension, each value on 1 to 48 neighbouring positions
- targets: int32 [2048], replicated, may hold values from 0 to 100351
- owners: int32 [64], replicated, may hold values from 0 to 63, each once
Outputs:
- hidden_out: bfloat16 [2, 2048, 2048], P(None, 'group', 'vocab')
- token_logprobs: float32 [2, 2048], P(None, 'group')
- seq_diff: float32 [64], P('group')
The draws below stay inside these ranges and needn't reach their ends.
Inputs may be any that keep to these rules, and one draw needn't show every extreme that they name: `page_table`: entry j of a request's row is a page held by group j mod (32); every page of the pool appears exactly once. `deal`: each request appears once. `owners`: each slot appears once. `segment_ids`: each row numbers its 2 sequences in order, every one present.
All inputs are finite; a program needn't handle non-finite values.
Results may differ from the reference program's by a relative error of at most 0.017.
The reference program's roundings to bfloat16 on the way (of `attended` and `final`) count: a program that leaves them out, or rounds other values in their place, can miss the bound.
Values may be sent and summed in bfloat16 or wider, within the bound.
No kernel may reach another device: no remote copies, remote signals or barrier semaphores. Data moves between devices by JAX's collectives and lax.ppermute only.
A program may use at most 192 MiB of HBM per device.

```python
import math
import jax
import jax.numpy as jnp
import numpy as np
from jax import lax

D = 2048
HEADS = 16
TOK_G = 64
SEQ_G = 2
PPG = 1
PAGE = 16
NREQ = 64
TOKENS = 2048
MAXP = 32
MAXLEN = 512
NPAGES = 2048
VOCAB = 100352
SEG_MOST = 48
N_GROUP = 32


def draw_page_table(key, part):
    groups = MAXP // PPG
    local_pages = NREQ * PPG
    keys = jax.random.split(jax.random.fold_in(key, 11), groups)

    def shuffle(one_key):
        return jax.random.permutation(one_key, local_pages)
    orders = jax.vmap(shuffle)(keys).astype(jnp.int32)
    base = jnp.arange(groups, dtype=jnp.int32)[:, None] * local_pages
    placed = (orders + base).reshape(groups, NREQ, PPG)
    return jnp.transpose(placed, (1, 2, 0)).reshape(NREQ, MAXP)


def draw_pool_keys(key, part):
    shape = (2, NPAGES, PAGE, D)
    return jnp.clip(jax.random.normal(key, shape, jnp.float32), -6.0, 6.0).astype(jnp.bfloat16)


def draw_head_weight(key, part):
    shape = (2, D, VOCAB)
    width_root = jnp.sqrt(jnp.float32(D))
    return (3.0 * jnp.clip(jax.random.normal(key, shape, jnp.float32), -6.0, 6.0) / width_root).astype(jnp.bfloat16)


def touch_ends(entries, key, smallest, largest):
    longest = entries.shape.index(max(entries.shape))
    spots = []
    for shift in (0, 1):
        where = [jax.random.randint(jax.random.fold_in(key, axis), (), 0, length) for axis, length in enumerate(entries.shape)]
        where[longest] = (where[longest] + shift) % entries.shape[longest]
        spots.append(tuple(where))
    return entries.at[spots[0]].set(smallest).at[spots[1]].set(largest)


def block_levels(rng, shape, pieces, least, largest):
    def one(position, blocks):
        steps = jax.random.uniform(jax.random.fold_in(jax.random.fold_in(rng, 6), position), (blocks,), jnp.float32, least / len(pieces), largest / len(pieces))
        return jnp.repeat(jnp.exp(steps), shape[position] // blocks).reshape((-1,) + (1,) * (len(shape) - position - 1))

    level = one(*pieces[0])
    for cut in pieces[1:]:
        level = level * one(*cut)
    return level


def ranked_wide(own_key, extent, count, lean):
    weights = [min(1 << octave, count + 1 - (1 << octave)) * (1 << 20) // math.isqrt((1 << octave) ** lean) + 1 for octave in range((count + 1).bit_length()) if 1 << octave <= count]
    width = 1 + sum(weights) // (1 << 30)
    listing = np.cumsum(np.array([max(1, weight // width) for weight in weights]))
    pick = jax.random.randint(jax.random.fold_in(own_key, 1), extent, 0, int(listing[len(weights) - 1]))
    start = jnp.left_shift(1, jnp.searchsorted(jnp.asarray(listing, jnp.int32), pick, side="right").astype(jnp.int32))
    rank = start - 1 + jax.random.randint(jax.random.fold_in(own_key, 4), extent, 0, 1 << 30) % jnp.minimum(start, count + 1 - start)
    return jax.random.permutation(jax.random.fold_in(own_key, 2), count)[rank].astype(jnp.int32)


def split_up(amount, total, reach, skew):
    portions = [(1 << 20) // math.isqrt(standing ** skew) + 1 for standing in range(2, amount + 1)]
    rest, given = total - reach - (amount - 1), [1] * (amount - 1)
    while rest > 0:
        free = [i for i in range(amount - 1) if given[i] < reach]
        mass, remaining = sum([portions[i] for i in free]), rest
        for i in free:
            more = min(reach - given[i], max(1, remaining * portions[i] // mass), rest)
            given[i] = given[i] + more
            rest = rest - more
    return np.array([reach] + given)


def ragged_sizes(stream_key, number_of, total, bound, slope):
    if number_of == 2:
        one = jax.random.randint(stream_key, (), max(1, total - bound), min(bound, total - 1) + 1)
        return jnp.stack([one, total - one])
    lengths = jnp.asarray(split_up(number_of, total, bound, slope), jnp.int32)
    pairs = (number_of - 1) // 2
    giver, sink = lengths[1:1 + 2 * pairs:2], lengths[2:2 + 2 * pairs:2]
    room = jnp.minimum(giver - 1, bound - sink)
    passed = jax.random.randint(jax.random.fold_in(stream_key, 1), (pairs,), 0, 1 << 20) % (room + 1)
    lengths = lengths.at[1:1 + 2 * pairs:2].set(giver - passed).at[2:2 + 2 * pairs:2].set(sink + passed)
    return lengths[jax.random.permutation(jax.random.fold_in(stream_key, 2), number_of)]


def gaussian(rng, shape, deviation, reach, pieces=(), kind=jnp.bfloat16):
    result = jax.random.normal(rng, shape, jnp.float32) * deviation
    if len(pieces) > 0:
        result = block_levels(rng, shape, pieces, -0.22, 0.18) * result
    return jnp.clip(result, min=-reach, max=reach).astype(kind)


def setup_inputs(seed: int = 0) -> dict:
    key_list = jax.random.split(jax.random.key(seed), 17)
    return {
        "hidden_in": gaussian(key_list[0], (2, TOKENS, D), 1.0, 6.0, ((1, 32),)),
        "qkv_weight": gaussian(key_list[1], (2, D, 3 * D), D ** -0.5, 0.125, ((1, 32), (2, 16))),
        "out_weight": gaussian(key_list[2], (2, D, D), D ** -0.5, 0.125, ((1, 16), (2, 32))),
        "q_gain": jnp.clip(1.0 + 0.18 * jax.random.normal(key_list[3], (2, D), jnp.float32), 0.1, 1.9),
        "k_gain": jnp.clip(1.0 + 0.18 * jax.random.normal(key_list[4], (2, D), jnp.float32), 0.1, 1.9),
        "post_gain": jnp.clip(1.0 + 0.18 * jax.random.normal(key_list[5], (2, D), jnp.float32), 0.1, 1.9),
        "final_gain": jnp.clip(1.0 + 0.18 * jax.random.normal(key_list[6], (2, D), jnp.float32), 0.1, 1.9),
        "head_weight": draw_head_weight(jax.random.fold_in(key_list[16], 71), 0),
        "pool_keys": draw_pool_keys(jax.random.fold_in(key_list[16], 71), 0),
        "pool_values": gaussian(key_list[9], (2, NPAGES, PAGE, D), 1.0, 6.0, ((1, 32), (3, 16))),
        "page_table": draw_page_table(jax.random.fold_in(key_list[16], 71), 0),
        "deal": jax.random.permutation(key_list[11], NREQ).astype(jnp.int32),
        "prompt_len": ragged_sizes(key_list[12], NREQ, NREQ * MAXLEN * 2 // 5, MAXLEN, 2).astype(jnp.int32),
        "segment_ids": jax.vmap(lambda own: jnp.searchsorted(jnp.cumsum(ragged_sizes(own, SEQ_G, TOK_G, SEG_MOST, 0)), jnp.arange(TOK_G), side="right"))(jax.random.split(key_list[13], N_GROUP)).reshape((N_GROUP, TOK_G)).astype(jnp.int32),
        "targets": touch_ends(ranked_wide(key_list[14], (TOKENS,), VOCAB, 2), jax.random.fold_in(key_list[14], 3), 0, VOCAB - 1).astype(jnp.int32),
        "owners": jax.random.permutation(key_list[15], NREQ).astype(jnp.int32),
    }


EPS = 1e-06
THETA = 500000.0
MASKED = -1e+30

def rms_scale(values, gain):
    mean_sq = lax.optimization_barrier(jnp.mean(values * values, axis=-1, keepdims=True))
    return values * lax.rsqrt(mean_sq + EPS) * gain

def rotate(values, positions):
    half = values.shape[-1] // 2
    freq = THETA ** (-(jnp.arange(half, dtype=jnp.float32) * 2.0 / values.shape[-1]))
    angle = positions[:, None] * freq[None, :]
    cosine = jnp.concatenate([jnp.cos(angle), jnp.cos(angle)], axis=-1)[:, None, :]
    sine = jnp.concatenate([jnp.sin(angle), jnp.sin(angle)], axis=-1)[:, None, :]
    rolled = jnp.concatenate([-values[..., half:], values[..., :half]], axis=-1)
    return values * cosine + rolled * sine

def reference(hidden_in, qkv_weight, out_weight, q_gain, k_gain, post_gain, final_gain, head_weight, pool_keys, pool_values, page_table, deal, prompt_len, segment_ids, targets, owners):
    head_size = D // HEADS
    score_scale = 1.0 / math.sqrt(head_size)
    united_weight = qkv_weight.astype(jnp.float32)
    out_matrix = out_weight.astype(jnp.float32)
    seq_numbers = jnp.arange(SEQ_G, dtype=jnp.int32)
    token_index = jnp.arange(TOK_G, dtype=jnp.int32)

    def one_group(group_idx):
        rows_in = lax.dynamic_slice_in_dim(hidden_in, group_idx * TOK_G, TOK_G, 1)
        seg_ids = segment_ids[group_idx]
        requests = lax.dynamic_slice_in_dim(deal, group_idx * SEQ_G, SEQ_G)
        prompt_rows = prompt_len[requests]
        onehot = seg_ids[:, None] == seq_numbers[None, :]
        starts = lax.optimization_barrier(jnp.sum((seg_ids[None, :] < seq_numbers[:, None]).astype(jnp.int32), axis=1))
        tok_start = lax.optimization_barrier(jnp.sum(jnp.where(onehot, starts[None, :], 0), axis=1))
        tok_prompt = lax.optimization_barrier(jnp.sum(jnp.where(onehot, prompt_rows[None, :], 0), axis=1))
        positions = (tok_prompt + token_index - tok_start).astype(jnp.float32)
        united = jnp.einsum('mtd,mdc->mtc', rows_in.astype(jnp.float32), united_weight).reshape(2, TOK_G, HEADS, 3, head_size)
        query_raw = united[:, :, :, 0, :].reshape(2, TOK_G, D)
        key_raw = united[:, :, :, 1, :].reshape(2, TOK_G, D)
        queries = rotate(rms_scale(query_raw, q_gain[:, None, :]).reshape(2, TOK_G, HEADS, head_size), positions).astype(jnp.bfloat16)
        new_keys = rotate(rms_scale(key_raw, k_gain[:, None, :]).reshape(2, TOK_G, HEADS, head_size), positions).astype(jnp.bfloat16)
        new_values = united[:, :, :, 2, :].astype(jnp.bfloat16)
        pages = page_table[requests]
        cache_keys = pool_keys[:, pages].reshape(2, SEQ_G, MAXLEN, HEADS, head_size).astype(jnp.float32)
        cache_values = pool_values[:, pages].reshape(2, SEQ_G, MAXLEN, HEADS, head_size).astype(jnp.float32)
        valid = jnp.arange(MAXLEN, dtype=jnp.int32)[None, :] < prompt_rows[:, None]
        cache_mask = (onehot[:, :, None] & valid[None, :, :])[None, :, None, :, :]
        query_wide = queries.astype(jnp.float32)
        cache_scores = jnp.einsum('mthd,mslhd->mthsl', query_wide, cache_keys) * score_scale
        cache_scores = jnp.where(cache_mask, cache_scores, MASKED)
        same_seq = (seg_ids[:, None] == seg_ids[None, :]) & (token_index[None, :] <= token_index[:, None])
        self_mask = same_seq[None, :, None, :]
        self_scores = jnp.einsum('mthd,muhd->mthu', query_wide, new_keys.astype(jnp.float32)) * score_scale
        self_scores = jnp.where(self_mask, self_scores, MASKED)
        highest = jnp.maximum(lax.optimization_barrier(jnp.max(cache_scores, axis=(3, 4))), lax.optimization_barrier(jnp.max(self_scores, axis=3)))
        cache_weights = jnp.where(cache_mask, jnp.exp(cache_scores - highest[..., None, None]), 0.0)
        self_weights = jnp.where(self_mask, jnp.exp(self_scores - highest[..., None]), 0.0)
        denominator = lax.optimization_barrier(jnp.sum(cache_weights, axis=(3, 4))) + lax.optimization_barrier(jnp.sum(self_weights, axis=3))
        weighted = jnp.einsum('mthsl,mslhd->mthd', cache_weights, cache_values) + jnp.einsum('mthu,muhd->mthd', self_weights, new_values.astype(jnp.float32))
        attended = (weighted / denominator[..., None]).reshape(2, TOK_G, D).astype(jnp.bfloat16)
        mixed = jnp.einsum('mtc,mcd->mtd', attended.astype(jnp.float32), out_matrix)
        hidden_new = (rows_in.astype(jnp.float32) + rms_scale(mixed, post_gain[:, None, :])).astype(jnp.bfloat16)
        final = rms_scale(hidden_new.astype(jnp.float32), final_gain[:, None, :]).astype(jnp.bfloat16)
        wanted = lax.dynamic_slice_in_dim(targets, group_idx * TOK_G, TOK_G)
        results = []
        for model in range(2):
            logits = jnp.dot(final[model], head_weight[model], preferred_element_type=jnp.float32)
            peak_logit = lax.optimization_barrier(jnp.max(logits, axis=-1))
            log_total = peak_logit + jnp.log(lax.optimization_barrier(jnp.sum(jnp.exp(logits - peak_logit[:, None]), axis=-1)))
            picked = jnp.take_along_axis(logits, wanted[:, None], axis=1)[:, 0]
            results.append(picked - log_total)
        logprobs = jnp.stack(results)
        gap = logprobs[0] - logprobs[1]
        counts = lax.optimization_barrier(jnp.sum(onehot.astype(jnp.float32), axis=0))
        means = lax.optimization_barrier(jnp.sum(jnp.where(onehot, gap[:, None], 0.0), axis=0)) / counts
        return (hidden_new, logprobs, means)
    hidden_all, logprob_all, mean_all = lax.map(one_group, jnp.arange(N_GROUP, dtype=jnp.int32))
    hidden_out = jnp.transpose(hidden_all, (1, 0, 2, 3)).reshape(2, TOKENS, D)
    token_logprobs = jnp.transpose(logprob_all, (1, 0, 2)).reshape(2, TOKENS)
    seq_diff = jnp.zeros((NREQ,), jnp.float32).at[owners[deal]].set(mean_all.reshape(NREQ))
    return (hidden_out, token_logprobs, seq_diff)
```

```python
import math

import jax
import jax.numpy as jnp
from jax import lax
from jax.sharding import PartitionSpec as P

D = 2048
HEADS = 16
TOK_G = 64
SEQ_G = 2
PPG = 1


EPS = 1e-06
THETA = 500000.0
MASKED = -1e30


def rms_scale(values, gain):
    mean_sq = jnp.mean(values * values, axis=-1, keepdims=True)
    return values * lax.rsqrt(mean_sq + EPS) * gain


def rotate(values, positions):
    half = values.shape[-1] // 2
    freq = THETA ** (-(jnp.arange(half, dtype=jnp.float32) * 2.0 / values.shape[-1]))
    angle = positions[:, None] * freq[None, :]
    cosine = jnp.concatenate([jnp.cos(angle), jnp.cos(angle)], axis=-1)[:, None, :]
    sine = jnp.concatenate([jnp.sin(angle), jnp.sin(angle)], axis=-1)[:, None, :]
    rolled = jnp.concatenate([-values[..., half:], values[..., :half]], axis=-1)
    return values * cosine + rolled * sine


def pick_small(table, index):
    match = jnp.arange(table.shape[0], dtype=jnp.int32)[None, :] == index[:, None]
    return jnp.sum(jnp.where(match, table[None, :], 0), axis=1)


def blend(first, second):
    top_one, mass_one, sum_one = first
    top_two, mass_two, sum_two = second
    highest = jnp.maximum(top_one, top_two)
    weight_one = jnp.exp(top_one - highest)
    weight_two = jnp.exp(top_two - highest)
    return (
        highest,
        mass_one * weight_one + mass_two * weight_two,
        sum_one * weight_one[..., None] + sum_two * weight_two[..., None],
    )


def shards(
    hidden_in,
    qkv_weight,
    out_weight,
    q_gain,
    k_gain,
    post_gain,
    final_gain,
    head_weight,
    pool_keys,
    pool_values,
    page_table,
    deal,
    prompt_len,
    segment_ids,
    targets,
    owners,
):
    groups = lax.axis_size("group")
    vocab_count = lax.axis_size("vocab")
    group_idx = lax.axis_index("group")
    vocab_idx = lax.axis_index("vocab")
    head_size = D // HEADS
    heads_dev = HEADS // vocab_count
    score_scale = 1.0 / math.sqrt(head_size)
    request_count = deal.shape[0]
    united = jnp.einsum(
        "mtd,mdc->mtc",
        hidden_in,
        lax.all_gather(qkv_weight, "group", axis=1, tiled=True),
        preferred_element_type=jnp.float32,
    )
    united = united.reshape(2, TOK_G, heads_dev, 3, head_size)
    query_raw = united[:, :, :, 0, :].reshape(2, TOK_G, heads_dev * head_size)
    key_raw = united[:, :, :, 1, :].reshape(2, TOK_G, heads_dev * head_size)
    query_sq, key_sq = lax.psum(
        (jnp.sum(query_raw * query_raw, axis=-1), jnp.sum(key_raw * key_raw, axis=-1)), "vocab"
    )
    query_normed = query_raw * lax.rsqrt(query_sq[..., None] / D + EPS) * q_gain[:, None, :]
    key_normed = key_raw * lax.rsqrt(key_sq[..., None] / D + EPS) * k_gain[:, None, :]
    seg_ids = lax.dynamic_index_in_dim(segment_ids, group_idx, 0, keepdims=False)
    requests = lax.dynamic_slice_in_dim(deal, group_idx * SEQ_G, SEQ_G)
    seq_numbers = jnp.arange(SEQ_G, dtype=jnp.int32)
    token_index = jnp.arange(TOK_G, dtype=jnp.int32)
    onehot = seg_ids[:, None] == seq_numbers[None, :]
    starts = jnp.sum((seg_ids[None, :] < seq_numbers[:, None]).astype(jnp.int32), axis=1)
    prompt_rows = pick_small(prompt_len, requests)
    tok_start = jnp.sum(jnp.where(onehot, starts[None, :], 0), axis=1)
    tok_prompt = jnp.sum(jnp.where(onehot, prompt_rows[None, :], 0), axis=1)
    positions = (tok_prompt + token_index - tok_start).astype(jnp.float32)
    queries = rotate(query_normed.reshape(2, TOK_G, heads_dev, head_size), positions).astype(
        jnp.bfloat16
    )
    new_keys = rotate(key_normed.reshape(2, TOK_G, heads_dev, head_size), positions).astype(
        jnp.bfloat16
    )
    new_values = united[:, :, :, 2, :].astype(jnp.bfloat16)
    pages_here = pool_keys.shape[1]
    dealt = jnp.take(page_table, deal, axis=0).reshape(groups, SEQ_G, PPG, groups)
    local_pages = (
        lax.dynamic_index_in_dim(dealt, group_idx, 3, keepdims=False) - group_idx * pages_here
    )
    order = jnp.transpose(local_pages, (1, 2, 0))
    send_keys = jnp.take(pool_keys, order, axis=1)
    send_values = jnp.take(pool_values, order, axis=1)
    got_keys, got_values = (
        lax.all_to_all(send_keys, "group", split_axis=3, concat_axis=3, tiled=True),
        lax.all_to_all(send_values, "group", split_axis=3, concat_axis=3, tiled=True),
    )
    cache_rows = got_keys.shape[2] * got_keys.shape[3] * got_keys.shape[4]
    cache_keys = got_keys.reshape(2, SEQ_G, cache_rows, heads_dev, head_size)
    cache_values = got_values.reshape(2, SEQ_G, cache_rows, heads_dev, head_size).astype(
        jnp.float32
    )
    valid = jnp.arange(cache_rows, dtype=jnp.int32)[None, :] < prompt_rows[:, None]
    cache_mask = (onehot[:, :, None] & valid[None, :, :])[None, :, None, :, :]
    cache_scores = (
        jnp.einsum("mthd,mslhd->mthsl", queries, cache_keys, preferred_element_type=jnp.float32)
        * score_scale
    )
    cache_scores = jnp.where(cache_mask, cache_scores, MASKED)
    peak_cache = jnp.max(cache_scores, axis=(3, 4))
    cache_weights = jnp.where(cache_mask, jnp.exp(cache_scores - peak_cache[..., None, None]), 0.0)
    mass_cache = jnp.sum(cache_weights, axis=(3, 4))
    sum_cache = jnp.einsum("mthsl,mslhd->mthd", cache_weights, cache_values)
    same_seq = (seg_ids[:, None] == seg_ids[None, :]) & (
        token_index[None, :] <= token_index[:, None]
    )
    self_mask = same_seq[None, :, None, :]
    self_scores = (
        jnp.einsum("mthd,muhd->mthu", queries, new_keys, preferred_element_type=jnp.float32)
        * score_scale
    )
    self_scores = jnp.where(self_mask, self_scores, MASKED)
    peak_self = jnp.max(self_scores, axis=3)
    self_weights = jnp.where(self_mask, jnp.exp(self_scores - peak_self[..., None]), 0.0)
    mass_self = jnp.sum(self_weights, axis=3)
    sum_self = jnp.einsum("mthu,muhd->mthd", self_weights, new_values.astype(jnp.float32))
    peak_both, mass_both, sum_both = blend(
        (peak_cache, mass_cache, sum_cache), (peak_self, mass_self, sum_self)
    )
    attended = (
        (sum_both / mass_both[..., None])
        .reshape(2, TOK_G, heads_dev * head_size)
        .astype(jnp.bfloat16)
    )
    partial_mix = jnp.einsum(
        "mtc,mcd->mtd",
        attended,
        lax.all_gather(out_weight, "group", axis=2, tiled=True),
        preferred_element_type=jnp.float32,
    )
    mixed = lax.psum(partial_mix, "vocab")
    hidden_new = (hidden_in.astype(jnp.float32) + rms_scale(mixed, post_gain[:, None, :])).astype(
        jnp.bfloat16
    )
    col_width = D // vocab_count
    hidden_out = lax.dynamic_slice_in_dim(hidden_new, vocab_idx * col_width, col_width, 2)
    final = rms_scale(hidden_new.astype(jnp.float32), final_gain[:, None, :]).astype(jnp.bfloat16)
    voc_here = head_weight.shape[2]
    first_column = (group_idx * vocab_count + vocab_idx) * voc_here
    logits = jnp.einsum(
        "mtd,mdv->mtv",
        lax.all_gather(final, "group", axis=1, tiled=True),
        head_weight,
        preferred_element_type=jnp.float32,
    )
    highest = jnp.max(logits, axis=-1)
    exp_sum = jnp.sum(jnp.exp(logits - highest[..., None]), axis=-1)
    wanted = targets - first_column
    found = jnp.arange(voc_here, dtype=jnp.int32)[None, :] == wanted[:, None]
    picked = jnp.sum(jnp.where(found[None], logits, 0.0), axis=-1)
    slot_numbers = jnp.arange(request_count, dtype=jnp.int32)
    request_of_slot = jnp.sum(
        jnp.where(owners[None, :] == slot_numbers[:, None], slot_numbers[None, :], 0), axis=1
    )
    place_of_slot = jnp.sum(
        jnp.where(deal[None, :] == request_of_slot[:, None], slot_numbers[None, :], 0), axis=1
    )
    group_of_slot = place_of_slot // SEQ_G
    seq_of_slot = place_of_slot % SEQ_G
    dest_groups = jnp.arange(groups, dtype=jnp.int32)
    slots_per_group = request_count // groups
    row_groups = jnp.concatenate(
        (dest_groups[:, None], group_of_slot.reshape(groups, slots_per_group)), axis=1
    )
    statistics = jnp.stack((highest, exp_sum, picked), axis=0).reshape(3, 2, groups, TOK_G)
    rows = jnp.take(statistics, row_groups.reshape(-1), axis=2).reshape(
        3, 2, groups, 1 + slots_per_group, TOK_G
    )
    rows = jnp.transpose(rows, (2, 3, 0, 1, 4))
    got = lax.all_to_all(rows, "group", split_axis=0, concat_axis=0, tiled=True)
    peak_one = jnp.max(got[:, :, 0], axis=0)
    mass_one = jnp.sum(got[:, :, 1] * jnp.exp(got[:, :, 0] - peak_one[None]), axis=0)
    target_one = jnp.sum(got[:, :, 2], axis=0)
    gathered = lax.all_gather(jnp.stack((peak_one, mass_one, target_one), axis=0), "vocab")
    peak_logit = jnp.max(gathered[:, 0], axis=0)
    exp_total = jnp.sum(gathered[:, 1] * jnp.exp(gathered[:, 0] - peak_logit[None]), axis=0)
    target_logit = jnp.sum(gathered[:, 2], axis=0)
    logprobs = target_logit - (peak_logit + jnp.log(exp_total))
    own_logprobs = logprobs[0]
    my_slots = group_idx * slots_per_group + jnp.arange(slots_per_group, dtype=jnp.int32)
    slot_groups = jnp.take(group_of_slot, my_slots)
    slot_seqs = jnp.take(seq_of_slot, my_slots)
    slot_ids = jnp.take(segment_ids, slot_groups, axis=0)
    in_seq = (slot_ids == slot_seqs[:, None]).astype(jnp.float32)
    slot_gap = logprobs[1:, 0] - logprobs[1:, 1]
    seq_diff = jnp.sum(in_seq * slot_gap, axis=1) / jnp.sum(in_seq, axis=1)
    return (hidden_out, own_logprobs, seq_diff)


def solution(mesh):
    return jax.shard_map(
        shards,
        mesh=mesh,
        in_specs=(
            P(None, "group", None),
            P(None, "group", "vocab"),
            P(None, "vocab", "group"),
            P(None, "vocab"),
            P(None, "vocab"),
            P(),
            P(),
            P(None, None, ("group", "vocab")),
            P(None, "group", None, "vocab"),
            P(None, "group", None, "vocab"),
            P(),
            P(),
            P(),
            P(),
            P(),
            P(),
        ),
        out_specs=(P(None, "group", "vocab"), P(None, "group"), P("group")),
        check_vma=False,
    )
```

```python
import math

import jax
import jax.numpy as jnp
from jax import lax
from jax.sharding import PartitionSpec as P

D = 2048
HEADS = 16
TOK_G = 64
SEQ_G = 2
PPG = 1


EPS = 1e-06
THETA = 500000.0
MASKED = -1e30


def rms_scale(values, gain):
    mean_sq = jnp.mean(values * values, axis=-1, keepdims=True)
    return values * lax.rsqrt(mean_sq + EPS) * gain


def rotate(values, positions):
    half = values.shape[-1] // 2
    freq = THETA ** (-(jnp.arange(half, dtype=jnp.float32) * 2.0 / values.shape[-1]))
    angle = positions[:, None] * freq[None, :]
    cosine = jnp.concatenate([jnp.cos(angle), jnp.cos(angle)], axis=-1)[:, None, :]
    sine = jnp.concatenate([jnp.sin(angle), jnp.sin(angle)], axis=-1)[:, None, :]
    rolled = jnp.concatenate([-values[..., half:], values[..., :half]], axis=-1)
    return values * cosine + rolled * sine


def pick_small(table, index):
    match = jnp.arange(table.shape[0], dtype=jnp.int32)[None, :] == index[:, None]
    return jnp.sum(jnp.where(match, table[None, :], 0), axis=1)


def blend(first, second):
    top_one, mass_one, sum_one = first
    top_two, mass_two, sum_two = second
    highest = jnp.maximum(top_one, top_two)
    weight_one = jnp.exp(top_one - highest)
    weight_two = jnp.exp(top_two - highest)
    return (
        highest,
        mass_one * weight_one + mass_two * weight_two,
        sum_one * weight_one[..., None] + sum_two * weight_two[..., None],
    )


def shards(
    hidden_in,
    qkv_weight,
    out_weight,
    q_gain,
    k_gain,
    post_gain,
    final_gain,
    head_weight,
    pool_keys,
    pool_values,
    page_table,
    deal,
    prompt_len,
    segment_ids,
    targets,
    owners,
):
    groups = lax.axis_size("group")
    vocab_count = lax.axis_size("vocab")
    group_idx = lax.axis_index("group")
    vocab_idx = lax.axis_index("vocab")
    head_size = D // HEADS
    heads_dev = HEADS // vocab_count
    score_scale = 1.0 / math.sqrt(head_size)
    request_count = deal.shape[0]
    united = jnp.einsum(
        "mtd,mdc->mtc",
        hidden_in,
        lax.all_gather(qkv_weight, "group", axis=1, tiled=True),
        preferred_element_type=jnp.float32,
    )
    united = united.reshape(2, TOK_G, heads_dev, 3, head_size)
    query_raw = united[:, :, :, 0, :].reshape(2, TOK_G, heads_dev * head_size)
    key_raw = united[:, :, :, 1, :].reshape(2, TOK_G, heads_dev * head_size)
    query_sq, key_sq = lax.psum(
        (jnp.sum(query_raw * query_raw, axis=-1), jnp.sum(key_raw * key_raw, axis=-1)), "vocab"
    )
    query_normed = query_raw * lax.rsqrt(query_sq[..., None] / D + EPS) * q_gain[:, None, :]
    key_normed = key_raw * lax.rsqrt(key_sq[..., None] / D + EPS) * k_gain[:, None, :]
    seg_ids = lax.dynamic_index_in_dim(segment_ids, group_idx, 0, keepdims=False)
    requests = lax.dynamic_slice_in_dim(deal, group_idx * SEQ_G, SEQ_G)
    seq_numbers = jnp.arange(SEQ_G, dtype=jnp.int32)
    token_index = jnp.arange(TOK_G, dtype=jnp.int32)
    onehot = seg_ids[:, None] == seq_numbers[None, :]
    starts = jnp.sum((seg_ids[None, :] < seq_numbers[:, None]).astype(jnp.int32), axis=1)
    prompt_rows = pick_small(prompt_len, requests)
    tok_start = jnp.sum(jnp.where(onehot, starts[None, :], 0), axis=1)
    tok_prompt = jnp.sum(jnp.where(onehot, prompt_rows[None, :], 0), axis=1)
    positions = (tok_prompt + token_index - tok_start).astype(jnp.float32)
    queries = rotate(query_normed.reshape(2, TOK_G, heads_dev, head_size), positions).astype(
        jnp.bfloat16
    )
    new_keys = rotate(key_normed.reshape(2, TOK_G, heads_dev, head_size), positions).astype(
        jnp.bfloat16
    )
    new_values = united[:, :, :, 2, :].astype(jnp.bfloat16)
    pages_here = pool_keys.shape[1]
    dealt = jnp.take(page_table, deal, axis=0).reshape(groups, SEQ_G, PPG, groups)
    local_pages = (
        lax.dynamic_index_in_dim(dealt, group_idx, 3, keepdims=False) - group_idx * pages_here
    )
    order = jnp.transpose(local_pages, (1, 2, 0))
    send_keys = jnp.take(pool_keys, order, axis=1)
    send_values = jnp.take(pool_values, order, axis=1)
    got_keys, got_values = (
        lax.all_to_all(send_keys, "group", split_axis=3, concat_axis=3, tiled=True),
        lax.all_to_all(send_values, "group", split_axis=3, concat_axis=3, tiled=True),
    )
    cache_rows = got_keys.shape[2] * got_keys.shape[3] * got_keys.shape[4]
    cache_keys = got_keys.reshape(2, SEQ_G, cache_rows, heads_dev, head_size)
    cache_values = got_values.reshape(2, SEQ_G, cache_rows, heads_dev, head_size).astype(
        jnp.float32
    )
    valid = jnp.arange(cache_rows, dtype=jnp.int32)[None, :] < prompt_rows[:, None]
    cache_mask = (onehot[:, :, None] & valid[None, :, :])[None, :, None, :, :]
    cache_scores = (
        jnp.einsum("mthd,mslhd->mthsl", queries, cache_keys, preferred_element_type=jnp.float32)
        * score_scale
    )
    cache_scores = jnp.where(cache_mask, cache_scores, MASKED)
    peak_cache = jnp.max(cache_scores, axis=(3, 4))
    cache_weights = jnp.where(cache_mask, jnp.exp(cache_scores - peak_cache[..., None, None]), 0.0)
    mass_cache = jnp.sum(cache_weights, axis=(3, 4))
    sum_cache = jnp.einsum("mthsl,mslhd->mthd", cache_weights, cache_values)
    same_seq = (seg_ids[:, None] == seg_ids[None, :]) & (
        token_index[None, :] <= token_index[:, None]
    )
    self_mask = same_seq[None, :, None, :]
    self_scores = (
        jnp.einsum("mthd,muhd->mthu", queries, new_keys, preferred_element_type=jnp.float32)
        * score_scale
    )
    self_scores = jnp.where(self_mask, self_scores, MASKED)
    peak_self = jnp.max(self_scores, axis=3)
    self_weights = jnp.where(self_mask, jnp.exp(self_scores - peak_self[..., None]), 0.0)
    mass_self = jnp.sum(self_weights, axis=3)
    sum_self = jnp.einsum("mthu,muhd->mthd", self_weights, new_values.astype(jnp.float32))
    peak_both, mass_both, sum_both = blend(
        (peak_cache, mass_cache, sum_cache), (peak_self, mass_self, sum_self)
    )
    attended = (
        (sum_both / mass_both[..., None])
        .reshape(2, TOK_G, heads_dev * head_size)
        .astype(jnp.bfloat16)
    )
    partial_mix = jnp.einsum(
        "mtc,mcd->mtd",
        attended,
        lax.all_gather(out_weight, "group", axis=2, tiled=True),
        preferred_element_type=jnp.float32,
    )
    mixed = lax.psum(partial_mix.astype(jnp.bfloat16), "vocab").astype(jnp.float32)
    hidden_new = (hidden_in.astype(jnp.float32) + rms_scale(mixed, post_gain[:, None, :])).astype(
        jnp.bfloat16
    )
    col_width = D // vocab_count
    hidden_out = lax.dynamic_slice_in_dim(hidden_new, vocab_idx * col_width, col_width, 2)
    final = rms_scale(hidden_new.astype(jnp.float32), final_gain[:, None, :]).astype(jnp.bfloat16)
    voc_here = head_weight.shape[2]
    first_column = (group_idx * vocab_count + vocab_idx) * voc_here
    logits = jnp.einsum(
        "mtd,mdv->mtv",
        lax.all_gather(final, "group", axis=1, tiled=True),
        head_weight,
        preferred_element_type=jnp.float32,
    )
    highest = jnp.max(logits, axis=-1)
    exp_sum = jnp.sum(jnp.exp(logits - highest[..., None]), axis=-1)
    wanted = targets - first_column
    found = jnp.arange(voc_here, dtype=jnp.int32)[None, :] == wanted[:, None]
    picked = jnp.sum(jnp.where(found[None], logits, 0.0), axis=-1)
    slot_numbers = jnp.arange(request_count, dtype=jnp.int32)
    request_of_slot = jnp.sum(
        jnp.where(owners[None, :] == slot_numbers[:, None], slot_numbers[None, :], 0), axis=1
    )
    place_of_slot = jnp.sum(
        jnp.where(deal[None, :] == request_of_slot[:, None], slot_numbers[None, :], 0), axis=1
    )
    group_of_slot = place_of_slot // SEQ_G
    seq_of_slot = place_of_slot % SEQ_G
    dest_groups = jnp.arange(groups, dtype=jnp.int32)
    slots_per_group = request_count // groups
    row_groups = jnp.concatenate(
        (dest_groups[:, None], group_of_slot.reshape(groups, slots_per_group)), axis=1
    )
    statistics = jnp.stack((highest, exp_sum, picked), axis=0).reshape(3, 2, groups, TOK_G)
    rows = jnp.take(statistics, row_groups.reshape(-1), axis=2).reshape(
        3, 2, groups, 1 + slots_per_group, TOK_G
    )
    rows = jnp.transpose(rows, (2, 3, 0, 1, 4))
    got = lax.all_to_all(rows, "group", split_axis=0, concat_axis=0, tiled=True)
    peak_one = jnp.max(got[:, :, 0], axis=0)
    mass_one = jnp.sum(got[:, :, 1] * jnp.exp(got[:, :, 0] - peak_one[None]), axis=0)
    target_one = jnp.sum(got[:, :, 2], axis=0)
    gathered = lax.all_gather(jnp.stack((peak_one, mass_one, target_one), axis=0), "vocab")
    peak_logit = jnp.max(gathered[:, 0], axis=0)
    exp_total = jnp.sum(gathered[:, 1] * jnp.exp(gathered[:, 0] - peak_logit[None]), axis=0)
    target_logit = jnp.sum(gathered[:, 2], axis=0)
    logprobs = target_logit - (peak_logit + jnp.log(exp_total))
    own_logprobs = logprobs[0]
    my_slots = group_idx * slots_per_group + jnp.arange(slots_per_group, dtype=jnp.int32)
    slot_groups = jnp.take(group_of_slot, my_slots)
    slot_seqs = jnp.take(seq_of_slot, my_slots)
    slot_ids = jnp.take(segment_ids, slot_groups, axis=0)
    in_seq = (slot_ids == slot_seqs[:, None]).astype(jnp.float32)
    slot_gap = logprobs[1:, 0] - logprobs[1:, 1]
    seq_diff = jnp.sum(in_seq * slot_gap, axis=1) / jnp.sum(in_seq, axis=1)
    return (hidden_out, own_logprobs, seq_diff)


def solution(mesh):
    return jax.shard_map(
        shards,
        mesh=mesh,
        in_specs=(
            P(None, "group", None),
            P(None, "group", "vocab"),
            P(None, "vocab", "group"),
            P(None, "vocab"),
            P(None, "vocab"),
            P(),
            P(),
            P(None, None, ("group", "vocab")),
            P(None, "group", None, "vocab"),
            P(None, "group", None, "vocab"),
            P(),
            P(),
            P(),
            P(),
            P(),
            P(),
        ),
        out_specs=(P(None, "group", "vocab"), P(None, "group"), P("group")),
        check_vma=False,
    )
```

```python
import math

import jax
import jax.numpy as jnp
from jax import lax
from jax.sharding import PartitionSpec as P

D = 2048
HEADS = 16
TOK_G = 64
SEQ_G = 2
PPG = 1


EPS = 1e-06
THETA = 500000.0
MASKED = -1e30


def rms_scale(values, gain):
    mean_sq = jnp.mean(values * values, axis=-1, keepdims=True)
    return values * lax.rsqrt(mean_sq + EPS) * gain


def rotate(values, positions):
    half = values.shape[-1] // 2
    freq = THETA ** (-(jnp.arange(half, dtype=jnp.float32) * 2.0 / values.shape[-1]))
    angle = positions[:, None] * freq[None, :]
    cosine = jnp.concatenate([jnp.cos(angle), jnp.cos(angle)], axis=-1)[:, None, :]
    sine = jnp.concatenate([jnp.sin(angle), jnp.sin(angle)], axis=-1)[:, None, :]
    rolled = jnp.concatenate([-values[..., half:], values[..., :half]], axis=-1)
    return values * cosine + rolled * sine


def pick_small(table, index):
    match = jnp.arange(table.shape[0], dtype=jnp.int32)[None, :] == index[:, None]
    return jnp.sum(jnp.where(match, table[None, :], 0), axis=1)


def blend(first, second):
    top_one, mass_one, sum_one = first
    top_two, mass_two, sum_two = second
    highest = jnp.maximum(top_one, top_two)
    weight_one = jnp.exp(top_one - highest)
    weight_two = jnp.exp(top_two - highest)
    return (
        highest,
        mass_one * weight_one + mass_two * weight_two,
        sum_one * weight_one[..., None] + sum_two * weight_two[..., None],
    )


def shards(
    hidden_in,
    qkv_weight,
    out_weight,
    q_gain,
    k_gain,
    post_gain,
    final_gain,
    head_weight,
    pool_keys,
    pool_values,
    page_table,
    deal,
    prompt_len,
    segment_ids,
    targets,
    owners,
):
    groups = lax.axis_size("group")
    vocab_count = lax.axis_size("vocab")
    group_idx = lax.axis_index("group")
    vocab_idx = lax.axis_index("vocab")
    head_size = D // HEADS
    heads_dev = HEADS // vocab_count
    score_scale = 1.0 / math.sqrt(head_size)
    request_count = deal.shape[0]
    qkv_rows = lax.all_gather(qkv_weight, "group", axis=1, tiled=True)
    qkv_rows, out_weight = lax.optimization_barrier((qkv_rows, out_weight))
    united = jnp.einsum("mtd,mdc->mtc", hidden_in, qkv_rows, preferred_element_type=jnp.float32)
    united = united.reshape(2, TOK_G, heads_dev, 3, head_size)
    query_raw = united[:, :, :, 0, :].reshape(2, TOK_G, heads_dev * head_size)
    key_raw = united[:, :, :, 1, :].reshape(2, TOK_G, heads_dev * head_size)
    query_sq, key_sq = lax.psum(
        (jnp.sum(query_raw * query_raw, axis=-1), jnp.sum(key_raw * key_raw, axis=-1)), "vocab"
    )
    query_normed = query_raw * lax.rsqrt(query_sq[..., None] / D + EPS) * q_gain[:, None, :]
    key_normed = key_raw * lax.rsqrt(key_sq[..., None] / D + EPS) * k_gain[:, None, :]
    seg_ids = lax.dynamic_index_in_dim(segment_ids, group_idx, 0, keepdims=False)
    requests = lax.dynamic_slice_in_dim(deal, group_idx * SEQ_G, SEQ_G)
    seq_numbers = jnp.arange(SEQ_G, dtype=jnp.int32)
    token_index = jnp.arange(TOK_G, dtype=jnp.int32)
    onehot = seg_ids[:, None] == seq_numbers[None, :]
    starts = jnp.sum((seg_ids[None, :] < seq_numbers[:, None]).astype(jnp.int32), axis=1)
    prompt_rows = pick_small(prompt_len, requests)
    tok_start = jnp.sum(jnp.where(onehot, starts[None, :], 0), axis=1)
    tok_prompt = jnp.sum(jnp.where(onehot, prompt_rows[None, :], 0), axis=1)
    positions = (tok_prompt + token_index - tok_start).astype(jnp.float32)
    queries = rotate(query_normed.reshape(2, TOK_G, heads_dev, head_size), positions).astype(
        jnp.bfloat16
    )
    new_keys = rotate(key_normed.reshape(2, TOK_G, heads_dev, head_size), positions).astype(
        jnp.bfloat16
    )
    new_values = united[:, :, :, 2, :].astype(jnp.bfloat16)
    pages_here = pool_keys.shape[1]
    dealt = jnp.take(page_table, deal, axis=0).reshape(groups, SEQ_G, PPG, groups)
    local_pages = (
        lax.dynamic_index_in_dim(dealt, group_idx, 3, keepdims=False) - group_idx * pages_here
    )
    order = jnp.transpose(local_pages, (1, 2, 0))
    send_keys = jnp.take(pool_keys, order, axis=1)
    send_values = jnp.take(pool_values, order, axis=1)
    got_keys, got_values = (
        lax.all_to_all(send_keys, "group", split_axis=3, concat_axis=3, tiled=True),
        lax.all_to_all(send_values, "group", split_axis=3, concat_axis=3, tiled=True),
    )
    cache_rows = got_keys.shape[2] * got_keys.shape[3] * got_keys.shape[4]
    cache_keys = got_keys.reshape(2, SEQ_G, cache_rows, heads_dev, head_size)
    cache_values = got_values.reshape(2, SEQ_G, cache_rows, heads_dev, head_size).astype(
        jnp.float32
    )
    valid = jnp.arange(cache_rows, dtype=jnp.int32)[None, :] < prompt_rows[:, None]
    cache_mask = (onehot[:, :, None] & valid[None, :, :])[None, :, None, :, :]
    cache_scores = (
        jnp.einsum("mthd,mslhd->mthsl", queries, cache_keys, preferred_element_type=jnp.float32)
        * score_scale
    )
    cache_scores = jnp.where(cache_mask, cache_scores, MASKED)
    peak_cache = jnp.max(cache_scores, axis=(3, 4))
    cache_weights = jnp.where(cache_mask, jnp.exp(cache_scores - peak_cache[..., None, None]), 0.0)
    mass_cache = jnp.sum(cache_weights, axis=(3, 4))
    sum_cache = jnp.einsum("mthsl,mslhd->mthd", cache_weights, cache_values)
    same_seq = (seg_ids[:, None] == seg_ids[None, :]) & (
        token_index[None, :] <= token_index[:, None]
    )
    self_mask = same_seq[None, :, None, :]
    self_scores = (
        jnp.einsum("mthd,muhd->mthu", queries, new_keys, preferred_element_type=jnp.float32)
        * score_scale
    )
    self_scores = jnp.where(self_mask, self_scores, MASKED)
    peak_self = jnp.max(self_scores, axis=3)
    self_weights = jnp.where(self_mask, jnp.exp(self_scores - peak_self[..., None]), 0.0)
    mass_self = jnp.sum(self_weights, axis=3)
    sum_self = jnp.einsum("mthu,muhd->mthd", self_weights, new_values.astype(jnp.float32))
    peak_both, mass_both, sum_both = blend(
        (peak_cache, mass_cache, sum_cache), (peak_self, mass_self, sum_self)
    )
    attended = (
        (sum_both / mass_both[..., None])
        .reshape(2, TOK_G, heads_dev * head_size)
        .astype(jnp.bfloat16)
    )
    col_width = D // vocab_count
    head_rows = lax.all_gather(out_weight, "group", axis=2, tiled=True)
    head_rows = jnp.transpose(
        head_rows.reshape(2, heads_dev * head_size, vocab_count, col_width), (2, 0, 1, 3)
    )
    column_block = lax.all_to_all(head_rows, "vocab", split_axis=0, concat_axis=0, tiled=True)
    column_block = jnp.transpose(column_block, (1, 0, 2, 3)).reshape(2, D, col_width)
    attended_all = lax.all_gather(attended, "vocab", axis=2, tiled=True)
    mixed_block = jnp.einsum(
        "mtc,mcd->mtd", attended_all, column_block, preferred_element_type=jnp.float32
    )
    mixed = lax.all_gather(mixed_block, "vocab", axis=2, tiled=True)
    hidden_new = (hidden_in.astype(jnp.float32) + rms_scale(mixed, post_gain[:, None, :])).astype(
        jnp.bfloat16
    )
    hidden_out = lax.dynamic_slice_in_dim(hidden_new, vocab_idx * col_width, col_width, 2)
    final = rms_scale(hidden_new.astype(jnp.float32), final_gain[:, None, :]).astype(jnp.bfloat16)
    voc_here = head_weight.shape[2]
    first_column = (group_idx * vocab_count + vocab_idx) * voc_here
    logits = jnp.einsum(
        "mtd,mdv->mtv",
        lax.all_gather(final, "group", axis=1, tiled=True),
        head_weight,
        preferred_element_type=jnp.float32,
    )
    highest = jnp.max(logits, axis=-1)
    exp_sum = jnp.sum(jnp.exp(logits - highest[..., None]), axis=-1)
    wanted = targets - first_column
    found = jnp.arange(voc_here, dtype=jnp.int32)[None, :] == wanted[:, None]
    picked = jnp.sum(jnp.where(found[None], logits, 0.0), axis=-1)
    slot_numbers = jnp.arange(request_count, dtype=jnp.int32)
    request_of_slot = jnp.sum(
        jnp.where(owners[None, :] == slot_numbers[:, None], slot_numbers[None, :], 0), axis=1
    )
    place_of_slot = jnp.sum(
        jnp.where(deal[None, :] == request_of_slot[:, None], slot_numbers[None, :], 0), axis=1
    )
    group_of_slot = place_of_slot // SEQ_G
    seq_of_slot = place_of_slot % SEQ_G
    dest_groups = jnp.arange(groups, dtype=jnp.int32)
    slots_per_group = request_count // groups
    row_groups = jnp.concatenate(
        (dest_groups[:, None], group_of_slot.reshape(groups, slots_per_group)), axis=1
    )
    statistics = jnp.stack((highest, exp_sum, picked), axis=0).reshape(3, 2, groups, TOK_G)
    rows = jnp.take(statistics, row_groups.reshape(-1), axis=2).reshape(
        3, 2, groups, 1 + slots_per_group, TOK_G
    )
    rows = jnp.transpose(rows, (2, 3, 0, 1, 4))
    got = lax.all_to_all(rows, "group", split_axis=0, concat_axis=0, tiled=True)
    peak_one = jnp.max(got[:, :, 0], axis=0)
    mass_one = jnp.sum(got[:, :, 1] * jnp.exp(got[:, :, 0] - peak_one[None]), axis=0)
    target_one = jnp.sum(got[:, :, 2], axis=0)
    gathered = lax.all_gather(jnp.stack((peak_one, mass_one, target_one), axis=0), "vocab")
    peak_logit = jnp.max(gathered[:, 0], axis=0)
    exp_total = jnp.sum(gathered[:, 1] * jnp.exp(gathered[:, 0] - peak_logit[None]), axis=0)
    target_logit = jnp.sum(gathered[:, 2], axis=0)
    logprobs = target_logit - (peak_logit + jnp.log(exp_total))
    own_logprobs = logprobs[0]
    my_slots = group_idx * slots_per_group + jnp.arange(slots_per_group, dtype=jnp.int32)
    slot_groups = jnp.take(group_of_slot, my_slots)
    slot_seqs = jnp.take(seq_of_slot, my_slots)
    slot_ids = jnp.take(segment_ids, slot_groups, axis=0)
    in_seq = (slot_ids == slot_seqs[:, None]).astype(jnp.float32)
    slot_gap = logprobs[1:, 0] - logprobs[1:, 1]
    seq_diff = jnp.sum(in_seq * slot_gap, axis=1) / jnp.sum(in_seq, axis=1)
    return (hidden_out, own_logprobs, seq_diff)


def solution(mesh):
    return jax.shard_map(
        shards,
        mesh=mesh,
        in_specs=(
            P(None, "group", None),
            P(None, "group", "vocab"),
            P(None, "vocab", "group"),
            P(None, "vocab"),
            P(None, "vocab"),
            P(),
            P(),
            P(None, None, ("group", "vocab")),
            P(None, "group", None, "vocab"),
            P(None, "group", None, "vocab"),
            P(),
            P(),
            P(),
            P(),
            P(),
            P(),
        ),
        out_specs=(P(None, "group", "vocab"), P(None, "group"), P("group")),
        check_vma=False,
    )
```

```python
import math

import jax
import jax.numpy as jnp
from jax import lax
from jax.sharding import PartitionSpec as P

D = 2048
HEADS = 16
TOK_G = 64
SEQ_G = 2
PPG = 1


EPS = 1e-06
THETA = 500000.0
MASKED = -1e30


def rms_scale(values, gain):
    mean_sq = jnp.mean(values * values, axis=-1, keepdims=True)
    return values * lax.rsqrt(mean_sq + EPS) * gain


def rotate(values, positions):
    half = values.shape[-1] // 2
    freq = THETA ** (-(jnp.arange(half, dtype=jnp.float32) * 2.0 / values.shape[-1]))
    angle = positions[:, None] * freq[None, :]
    cosine = jnp.concatenate([jnp.cos(angle), jnp.cos(angle)], axis=-1)[:, None, :]
    sine = jnp.concatenate([jnp.sin(angle), jnp.sin(angle)], axis=-1)[:, None, :]
    rolled = jnp.concatenate([-values[..., half:], values[..., :half]], axis=-1)
    return values * cosine + rolled * sine


def pick_small(table, index):
    match = jnp.arange(table.shape[0], dtype=jnp.int32)[None, :] == index[:, None]
    return jnp.sum(jnp.where(match, table[None, :], 0), axis=1)


def blend(first, second):
    top_one, mass_one, sum_one = first
    top_two, mass_two, sum_two = second
    highest = jnp.maximum(top_one, top_two)
    weight_one = jnp.exp(top_one - highest)
    weight_two = jnp.exp(top_two - highest)
    return (
        highest,
        mass_one * weight_one + mass_two * weight_two,
        sum_one * weight_one[..., None] + sum_two * weight_two[..., None],
    )


def shards(
    hidden_in,
    qkv_weight,
    out_weight,
    q_gain,
    k_gain,
    post_gain,
    final_gain,
    head_weight,
    pool_keys,
    pool_values,
    page_table,
    deal,
    prompt_len,
    segment_ids,
    targets,
    owners,
):
    groups = lax.axis_size("group")
    vocab_count = lax.axis_size("vocab")
    group_idx = lax.axis_index("group")
    vocab_idx = lax.axis_index("vocab")
    head_size = D // HEADS
    heads_dev = HEADS // vocab_count
    score_scale = 1.0 / math.sqrt(head_size)
    request_count = deal.shape[0]
    qkv_size = qkv_weight.size
    both_weights = lax.all_gather(
        jnp.concatenate((qkv_weight.reshape(-1), out_weight.reshape(-1))), "group"
    )
    qkv_rows = jnp.transpose(
        both_weights[:, :qkv_size].reshape((groups,) + qkv_weight.shape), (1, 0, 2, 3)
    ).reshape(2, groups * qkv_weight.shape[1], qkv_weight.shape[2])
    head_rows = jnp.transpose(
        both_weights[:, qkv_size:].reshape((groups,) + out_weight.shape), (1, 2, 0, 3)
    ).reshape(2, out_weight.shape[1], groups * out_weight.shape[2])
    united = jnp.einsum("mtd,mdc->mtc", hidden_in, qkv_rows, preferred_element_type=jnp.float32)
    united = united.reshape(2, TOK_G, heads_dev, 3, head_size)
    query_raw = united[:, :, :, 0, :].reshape(2, TOK_G, heads_dev * head_size)
    key_raw = united[:, :, :, 1, :].reshape(2, TOK_G, heads_dev * head_size)
    squares = lax.all_gather(
        jnp.stack((jnp.sum(query_raw * query_raw, axis=-1), jnp.sum(key_raw * key_raw, axis=-1))),
        "vocab",
    )
    query_sq = jnp.sum(squares[:, 0], axis=0)
    key_sq = jnp.sum(squares[:, 1], axis=0)
    query_normed = query_raw * lax.rsqrt(query_sq[..., None] / D + EPS) * q_gain[:, None, :]
    key_normed = key_raw * lax.rsqrt(key_sq[..., None] / D + EPS) * k_gain[:, None, :]
    seg_ids = lax.dynamic_index_in_dim(segment_ids, group_idx, 0, keepdims=False)
    requests = lax.dynamic_slice_in_dim(deal, group_idx * SEQ_G, SEQ_G)
    seq_numbers = jnp.arange(SEQ_G, dtype=jnp.int32)
    token_index = jnp.arange(TOK_G, dtype=jnp.int32)
    onehot = seg_ids[:, None] == seq_numbers[None, :]
    starts = jnp.sum((seg_ids[None, :] < seq_numbers[:, None]).astype(jnp.int32), axis=1)
    prompt_rows = pick_small(prompt_len, requests)
    tok_start = jnp.sum(jnp.where(onehot, starts[None, :], 0), axis=1)
    tok_prompt = jnp.sum(jnp.where(onehot, prompt_rows[None, :], 0), axis=1)
    positions = (tok_prompt + token_index - tok_start).astype(jnp.float32)
    queries = rotate(query_normed.reshape(2, TOK_G, heads_dev, head_size), positions).astype(
        jnp.bfloat16
    )
    new_keys = rotate(key_normed.reshape(2, TOK_G, heads_dev, head_size), positions).astype(
        jnp.bfloat16
    )
    new_values = united[:, :, :, 2, :].astype(jnp.bfloat16)
    pages_here = pool_keys.shape[1]
    dealt = jnp.take(page_table, deal, axis=0).reshape(groups, SEQ_G, PPG, groups)
    local_pages = (
        lax.dynamic_index_in_dim(dealt, group_idx, 3, keepdims=False) - group_idx * pages_here
    )
    order = jnp.transpose(local_pages, (1, 2, 0))
    send_keys = jnp.take(pool_keys, order, axis=1)
    send_values = jnp.take(pool_values, order, axis=1)
    got_keys, got_values = (
        lax.all_to_all(send_keys, "group", split_axis=3, concat_axis=3, tiled=True),
        lax.all_to_all(send_values, "group", split_axis=3, concat_axis=3, tiled=True),
    )
    cache_rows = got_keys.shape[2] * got_keys.shape[3] * got_keys.shape[4]
    cache_keys = got_keys.reshape(2, SEQ_G, cache_rows, heads_dev, head_size)
    cache_values = got_values.reshape(2, SEQ_G, cache_rows, heads_dev, head_size).astype(
        jnp.float32
    )
    valid = jnp.arange(cache_rows, dtype=jnp.int32)[None, :] < prompt_rows[:, None]
    cache_mask = (onehot[:, :, None] & valid[None, :, :])[None, :, None, :, :]
    cache_scores = (
        jnp.einsum("mthd,mslhd->mthsl", queries, cache_keys, preferred_element_type=jnp.float32)
        * score_scale
    )
    cache_scores = jnp.where(cache_mask, cache_scores, MASKED)
    peak_cache = jnp.max(cache_scores, axis=(3, 4))
    cache_weights = jnp.where(cache_mask, jnp.exp(cache_scores - peak_cache[..., None, None]), 0.0)
    mass_cache = jnp.sum(cache_weights, axis=(3, 4))
    sum_cache = jnp.einsum("mthsl,mslhd->mthd", cache_weights, cache_values)
    same_seq = (seg_ids[:, None] == seg_ids[None, :]) & (
        token_index[None, :] <= token_index[:, None]
    )
    self_mask = same_seq[None, :, None, :]
    self_scores = (
        jnp.einsum("mthd,muhd->mthu", queries, new_keys, preferred_element_type=jnp.float32)
        * score_scale
    )
    self_scores = jnp.where(self_mask, self_scores, MASKED)
    peak_self = jnp.max(self_scores, axis=3)
    self_weights = jnp.where(self_mask, jnp.exp(self_scores - peak_self[..., None]), 0.0)
    mass_self = jnp.sum(self_weights, axis=3)
    sum_self = jnp.einsum("mthu,muhd->mthd", self_weights, new_values.astype(jnp.float32))
    peak_both, mass_both, sum_both = blend(
        (peak_cache, mass_cache, sum_cache), (peak_self, mass_self, sum_self)
    )
    attended = (
        (sum_both / mass_both[..., None])
        .reshape(2, TOK_G, heads_dev * head_size)
        .astype(jnp.bfloat16)
    )
    col_width = D // vocab_count
    head_rows = jnp.transpose(
        head_rows.reshape(2, heads_dev * head_size, vocab_count, col_width), (2, 0, 1, 3)
    )
    column_block = lax.all_to_all(head_rows, "vocab", split_axis=0, concat_axis=0, tiled=True)
    column_block = jnp.transpose(column_block, (1, 0, 2, 3)).reshape(2, D, col_width)
    attended_all = lax.all_gather(attended, "vocab", axis=2, tiled=True)
    mixed_block = jnp.einsum(
        "mtc,mcd->mtd", attended_all, column_block, preferred_element_type=jnp.float32
    )
    mixed = lax.all_gather(mixed_block, "vocab", axis=2, tiled=True)
    hidden_new = (hidden_in.astype(jnp.float32) + rms_scale(mixed, post_gain[:, None, :])).astype(
        jnp.bfloat16
    )
    hidden_out = lax.dynamic_slice_in_dim(hidden_new, vocab_idx * col_width, col_width, 2)
    final = rms_scale(hidden_new.astype(jnp.float32), final_gain[:, None, :]).astype(jnp.bfloat16)
    voc_here = head_weight.shape[2]
    first_column = (group_idx * vocab_count + vocab_idx) * voc_here
    logits = jnp.einsum(
        "mtd,mdv->mtv",
        lax.all_gather(final, "group", axis=1, tiled=True),
        head_weight,
        preferred_element_type=jnp.float32,
    )
    highest = jnp.max(logits, axis=-1)
    exp_sum = jnp.sum(jnp.exp(logits - highest[..., None]), axis=-1)
    wanted = targets - first_column
    found = jnp.arange(voc_here, dtype=jnp.int32)[None, :] == wanted[:, None]
    picked = jnp.sum(jnp.where(found[None], logits, 0.0), axis=-1)
    slot_numbers = jnp.arange(request_count, dtype=jnp.int32)
    request_of_slot = jnp.sum(
        jnp.where(owners[None, :] == slot_numbers[:, None], slot_numbers[None, :], 0), axis=1
    )
    place_of_slot = jnp.sum(
        jnp.where(deal[None, :] == request_of_slot[:, None], slot_numbers[None, :], 0), axis=1
    )
    group_of_slot = place_of_slot // SEQ_G
    seq_of_slot = place_of_slot % SEQ_G
    dest_groups = jnp.arange(groups, dtype=jnp.int32)
    slots_per_group = request_count // groups
    row_groups = jnp.concatenate(
        (dest_groups[:, None], group_of_slot.reshape(groups, slots_per_group)), axis=1
    )
    statistics = jnp.stack((highest, exp_sum, picked), axis=0).reshape(3, 2, groups, TOK_G)
    rows = jnp.take(statistics, row_groups.reshape(-1), axis=2).reshape(
        3, 2, groups, 1 + slots_per_group, TOK_G
    )
    rows = jnp.transpose(rows, (2, 3, 0, 1, 4))
    got = lax.all_to_all(rows, "group", split_axis=0, concat_axis=0, tiled=True)
    peak_one = jnp.max(got[:, :, 0], axis=0)
    mass_one = jnp.sum(got[:, :, 1] * jnp.exp(got[:, :, 0] - peak_one[None]), axis=0)
    target_one = jnp.sum(got[:, :, 2], axis=0)
    gathered = lax.all_gather(jnp.stack((peak_one, mass_one, target_one), axis=0), "vocab")
    peak_logit = jnp.max(gathered[:, 0], axis=0)
    exp_total = jnp.sum(gathered[:, 1] * jnp.exp(gathered[:, 0] - peak_logit[None]), axis=0)
    target_logit = jnp.sum(gathered[:, 2], axis=0)
    logprobs = target_logit - (peak_logit + jnp.log(exp_total))
    own_logprobs = logprobs[0]
    my_slots = group_idx * slots_per_group + jnp.arange(slots_per_group, dtype=jnp.int32)
    slot_groups = jnp.take(group_of_slot, my_slots)
    slot_seqs = jnp.take(seq_of_slot, my_slots)
    slot_ids = jnp.take(segment_ids, slot_groups, axis=0)
    in_seq = (slot_ids == slot_seqs[:, None]).astype(jnp.float32)
    slot_gap = logprobs[1:, 0] - logprobs[1:, 1]
    seq_diff = jnp.sum(in_seq * slot_gap, axis=1) / jnp.sum(in_seq, axis=1)
    return (hidden_out, own_logprobs, seq_diff)


def solution(mesh):
    return jax.shard_map(
        shards,
        mesh=mesh,
        in_specs=(
            P(None, "group", None),
            P(None, "group", "vocab"),
            P(None, "vocab", "group"),
            P(None, "vocab"),
            P(None, "vocab"),
            P(),
            P(),
            P(None, None, ("group", "vocab")),
            P(None, "group", None, "vocab"),
            P(None, "group", None, "vocab"),
            P(),
            P(),
            P(),
            P(),
            P(),
            P(),
        ),
        out_specs=(P(None, "group", "vocab"), P(None, "group"), P("group")),
        check_vma=False,
    )
```

```python
import math

import jax
import jax.numpy as jnp
from jax import lax
from jax.sharding import PartitionSpec as P

D = 2048
HEADS = 16
TOK_G = 64
SEQ_G = 2
PPG = 1


EPS = 1e-06
THETA = 500000.0
MASKED = -1e30


def rms_scale(values, gain):
    mean_sq = jnp.mean(values * values, axis=-1, keepdims=True)
    return values * lax.rsqrt(mean_sq + EPS) * gain


def rotate(values, positions):
    half = values.shape[-1] // 2
    freq = THETA ** (-(jnp.arange(half, dtype=jnp.float32) * 2.0 / values.shape[-1]))
    angle = positions[:, None] * freq[None, :]
    cosine = jnp.concatenate([jnp.cos(angle), jnp.cos(angle)], axis=-1)[:, None, :]
    sine = jnp.concatenate([jnp.sin(angle), jnp.sin(angle)], axis=-1)[:, None, :]
    rolled = jnp.concatenate([-values[..., half:], values[..., :half]], axis=-1)
    return values * cosine + rolled * sine


def pick_small(table, index):
    match = jnp.arange(table.shape[0], dtype=jnp.int32)[None, :] == index[:, None]
    return jnp.sum(jnp.where(match, table[None, :], 0), axis=1)


def blend(first, second):
    top_one, mass_one, sum_one = first
    top_two, mass_two, sum_two = second
    highest = jnp.maximum(top_one, top_two)
    weight_one = jnp.exp(top_one - highest)
    weight_two = jnp.exp(top_two - highest)
    return (
        highest,
        mass_one * weight_one + mass_two * weight_two,
        sum_one * weight_one[..., None] + sum_two * weight_two[..., None],
    )


def shards(
    hidden_in,
    qkv_weight,
    out_weight,
    q_gain,
    k_gain,
    post_gain,
    final_gain,
    head_weight,
    pool_keys,
    pool_values,
    page_table,
    deal,
    prompt_len,
    segment_ids,
    targets,
    owners,
):
    groups = lax.axis_size("group")
    vocab_count = lax.axis_size("vocab")
    group_idx = lax.axis_index("group")
    vocab_idx = lax.axis_index("vocab")
    head_size = D // HEADS
    heads_dev = HEADS // vocab_count
    score_scale = 1.0 / math.sqrt(head_size)
    request_count = deal.shape[0]
    lane = head_size
    parts = qkv_weight.shape[2] // lane
    rows_here = qkv_weight.shape[1]
    qkv_local = jnp.transpose(qkv_weight.reshape(2, rows_here, parts, lane), (0, 2, 1, 3))
    both_weights = lax.all_gather(
        jnp.concatenate(
            (qkv_local.reshape(2, parts * rows_here, lane), out_weight.reshape(2, -1, lane)), axis=1
        ),
        "group",
    )
    qkv_rows = both_weights[:, :, : parts * rows_here].reshape(groups, 2, parts, rows_here, lane)
    out_rows = both_weights[:, :, parts * rows_here :].reshape((groups,) + out_weight.shape)
    united = jnp.einsum(
        "mtgr,gmjrl->mtjl",
        hidden_in.reshape(2, TOK_G, groups, rows_here),
        qkv_rows,
        preferred_element_type=jnp.float32,
    )
    united = united.reshape(2, TOK_G, heads_dev, 3, head_size)
    query_raw = united[:, :, :, 0, :].reshape(2, TOK_G, heads_dev * head_size)
    key_raw = united[:, :, :, 1, :].reshape(2, TOK_G, heads_dev * head_size)
    squares = lax.all_gather(
        jnp.stack((jnp.sum(query_raw * query_raw, axis=-1), jnp.sum(key_raw * key_raw, axis=-1))),
        "vocab",
    )
    query_sq = jnp.sum(squares[:, 0], axis=0)
    key_sq = jnp.sum(squares[:, 1], axis=0)
    query_normed = query_raw * lax.rsqrt(query_sq[..., None] / D + EPS) * q_gain[:, None, :]
    key_normed = key_raw * lax.rsqrt(key_sq[..., None] / D + EPS) * k_gain[:, None, :]
    seg_ids = lax.dynamic_index_in_dim(segment_ids, group_idx, 0, keepdims=False)
    requests = lax.dynamic_slice_in_dim(deal, group_idx * SEQ_G, SEQ_G)
    seq_numbers = jnp.arange(SEQ_G, dtype=jnp.int32)
    token_index = jnp.arange(TOK_G, dtype=jnp.int32)
    onehot = seg_ids[:, None] == seq_numbers[None, :]
    starts = jnp.sum((seg_ids[None, :] < seq_numbers[:, None]).astype(jnp.int32), axis=1)
    prompt_rows = pick_small(prompt_len, requests)
    tok_start = jnp.sum(jnp.where(onehot, starts[None, :], 0), axis=1)
    tok_prompt = jnp.sum(jnp.where(onehot, prompt_rows[None, :], 0), axis=1)
    positions = (tok_prompt + token_index - tok_start).astype(jnp.float32)
    queries = rotate(query_normed.reshape(2, TOK_G, heads_dev, head_size), positions).astype(
        jnp.bfloat16
    )
    new_keys = rotate(key_normed.reshape(2, TOK_G, heads_dev, head_size), positions).astype(
        jnp.bfloat16
    )
    new_values = united[:, :, :, 2, :].astype(jnp.bfloat16)
    pages_here = pool_keys.shape[1]
    dealt = jnp.take(page_table, deal, axis=0).reshape(groups, SEQ_G, PPG, groups)
    local_pages = (
        lax.dynamic_index_in_dim(dealt, group_idx, 3, keepdims=False) - group_idx * pages_here
    )
    order = jnp.transpose(local_pages, (1, 2, 0))
    send_keys = jnp.take(pool_keys, order, axis=1)
    send_values = jnp.take(pool_values, order, axis=1)
    got_keys, got_values = (
        lax.all_to_all(send_keys, "group", split_axis=3, concat_axis=3, tiled=True),
        lax.all_to_all(send_values, "group", split_axis=3, concat_axis=3, tiled=True),
    )
    cache_rows = got_keys.shape[2] * got_keys.shape[3] * got_keys.shape[4]
    cache_keys = got_keys.reshape(2, SEQ_G, cache_rows, heads_dev, head_size)
    cache_values = got_values.reshape(2, SEQ_G, cache_rows, heads_dev, head_size).astype(
        jnp.float32
    )
    valid = jnp.arange(cache_rows, dtype=jnp.int32)[None, :] < prompt_rows[:, None]
    cache_mask = (onehot[:, :, None] & valid[None, :, :])[None, :, None, :, :]
    cache_scores = (
        jnp.einsum("mthd,mslhd->mthsl", queries, cache_keys, preferred_element_type=jnp.float32)
        * score_scale
    )
    cache_scores = jnp.where(cache_mask, cache_scores, MASKED)
    peak_cache = jnp.max(cache_scores, axis=(3, 4))
    cache_weights = jnp.where(cache_mask, jnp.exp(cache_scores - peak_cache[..., None, None]), 0.0)
    mass_cache = jnp.sum(cache_weights, axis=(3, 4))
    sum_cache = jnp.einsum("mthsl,mslhd->mthd", cache_weights, cache_values)
    same_seq = (seg_ids[:, None] == seg_ids[None, :]) & (
        token_index[None, :] <= token_index[:, None]
    )
    self_mask = same_seq[None, :, None, :]
    self_scores = (
        jnp.einsum("mthd,muhd->mthu", queries, new_keys, preferred_element_type=jnp.float32)
        * score_scale
    )
    self_scores = jnp.where(self_mask, self_scores, MASKED)
    peak_self = jnp.max(self_scores, axis=3)
    self_weights = jnp.where(self_mask, jnp.exp(self_scores - peak_self[..., None]), 0.0)
    mass_self = jnp.sum(self_weights, axis=3)
    sum_self = jnp.einsum("mthu,muhd->mthd", self_weights, new_values.astype(jnp.float32))
    peak_both, mass_both, sum_both = blend(
        (peak_cache, mass_cache, sum_cache), (peak_self, mass_self, sum_self)
    )
    attended = (
        (sum_both / mass_both[..., None])
        .reshape(2, TOK_G, heads_dev * head_size)
        .astype(jnp.bfloat16)
    )
    col_width = D // vocab_count
    pair = groups // vocab_count
    head_rows = jnp.transpose(
        out_rows.reshape((vocab_count, pair) + out_weight.shape), (0, 2, 3, 1, 4)
    ).reshape(vocab_count, 2, heads_dev * head_size, col_width)
    column_block = lax.all_to_all(head_rows, "vocab", split_axis=0, concat_axis=0, tiled=True)
    column_block = jnp.transpose(column_block, (1, 0, 2, 3)).reshape(2, D, col_width)
    attended_all = lax.all_gather(attended, "vocab", axis=2, tiled=True)
    mixed_block = jnp.einsum(
        "mtc,mcd->mtd", attended_all, column_block, preferred_element_type=jnp.float32
    )
    mixed = lax.all_gather(mixed_block, "vocab", axis=2, tiled=True)
    hidden_new = (hidden_in.astype(jnp.float32) + rms_scale(mixed, post_gain[:, None, :])).astype(
        jnp.bfloat16
    )
    hidden_out = lax.dynamic_slice_in_dim(hidden_new, vocab_idx * col_width, col_width, 2)
    final = rms_scale(hidden_new.astype(jnp.float32), final_gain[:, None, :]).astype(jnp.bfloat16)
    voc_here = head_weight.shape[2]
    first_column = (group_idx * vocab_count + vocab_idx) * voc_here
    logits = jnp.einsum(
        "mtd,mdv->mtv",
        lax.all_gather(final, "group", axis=1, tiled=True),
        head_weight,
        preferred_element_type=jnp.float32,
    )
    highest = jnp.max(logits, axis=-1)
    exp_sum = jnp.sum(jnp.exp(logits - highest[..., None]), axis=-1)
    wanted = targets - first_column
    found = jnp.arange(voc_here, dtype=jnp.int32)[None, :] == wanted[:, None]
    picked = jnp.sum(jnp.where(found[None], logits, 0.0), axis=-1)
    slot_numbers = jnp.arange(request_count, dtype=jnp.int32)
    request_of_slot = jnp.sum(
        jnp.where(owners[None, :] == slot_numbers[:, None], slot_numbers[None, :], 0), axis=1
    )
    place_of_slot = jnp.sum(
        jnp.where(deal[None, :] == request_of_slot[:, None], slot_numbers[None, :], 0), axis=1
    )
    group_of_slot = place_of_slot // SEQ_G
    seq_of_slot = place_of_slot % SEQ_G
    dest_groups = jnp.arange(groups, dtype=jnp.int32)
    slots_per_group = request_count // groups
    row_groups = jnp.concatenate(
        (dest_groups[:, None], group_of_slot.reshape(groups, slots_per_group)), axis=1
    )
    statistics = jnp.stack((highest, exp_sum, picked), axis=0).reshape(3, 2, groups, TOK_G)
    rows = jnp.take(statistics, row_groups.reshape(-1), axis=2).reshape(
        3, 2, groups, 1 + slots_per_group, TOK_G
    )
    rows = jnp.transpose(rows, (2, 3, 0, 1, 4))
    got = lax.all_to_all(rows, "group", split_axis=0, concat_axis=0, tiled=True)
    peak_one = jnp.max(got[:, :, 0], axis=0)
    mass_one = jnp.sum(got[:, :, 1] * jnp.exp(got[:, :, 0] - peak_one[None]), axis=0)
    target_one = jnp.sum(got[:, :, 2], axis=0)
    gathered = lax.all_gather(jnp.stack((peak_one, mass_one, target_one), axis=0), "vocab")
    peak_logit = jnp.max(gathered[:, 0], axis=0)
    exp_total = jnp.sum(gathered[:, 1] * jnp.exp(gathered[:, 0] - peak_logit[None]), axis=0)
    target_logit = jnp.sum(gathered[:, 2], axis=0)
    logprobs = target_logit - (peak_logit + jnp.log(exp_total))
    own_logprobs = logprobs[0]
    my_slots = group_idx * slots_per_group + jnp.arange(slots_per_group, dtype=jnp.int32)
    slot_groups = jnp.take(group_of_slot, my_slots)
    slot_seqs = jnp.take(seq_of_slot, my_slots)
    slot_ids = jnp.take(segment_ids, slot_groups, axis=0)
    in_seq = (slot_ids == slot_seqs[:, None]).astype(jnp.float32)
    slot_gap = logprobs[1:, 0] - logprobs[1:, 1]
    seq_diff = jnp.sum(in_seq * slot_gap, axis=1) / jnp.sum(in_seq, axis=1)
    return (hidden_out, own_logprobs, seq_diff)


def solution(mesh):
    return jax.shard_map(
        shards,
        mesh=mesh,
        in_specs=(
            P(None, "group", None),
            P(None, "group", "vocab"),
            P(None, "vocab", "group"),
            P(None, "vocab"),
            P(None, "vocab"),
            P(),
            P(),
            P(None, None, ("group", "vocab")),
            P(None, "group", None, "vocab"),
            P(None, "group", None, "vocab"),
            P(),
            P(),
            P(),
            P(),
            P(),
            P(),
        ),
        out_specs=(P(None, "group", "vocab"), P(None, "group"), P("group")),
        check_vma=False,
    )
```

```python
import math

import jax
import jax.numpy as jnp
from jax import lax
from jax.sharding import PartitionSpec as P

D = 2048
HEADS = 16
TOK_G = 64
SEQ_G = 2
PPG = 1


EPS = 1e-06
THETA = 500000.0
MASKED = -1e30


def rms_scale(values, gain):
    mean_sq = jnp.mean(values * values, axis=-1, keepdims=True)
    return values * lax.rsqrt(mean_sq + EPS) * gain


def rotate(values, positions):
    half = values.shape[-1] // 2
    freq = THETA ** (-(jnp.arange(half, dtype=jnp.float32) * 2.0 / values.shape[-1]))
    angle = positions[:, None] * freq[None, :]
    cosine = jnp.concatenate([jnp.cos(angle), jnp.cos(angle)], axis=-1)[:, None, :]
    sine = jnp.concatenate([jnp.sin(angle), jnp.sin(angle)], axis=-1)[:, None, :]
    rolled = jnp.concatenate([-values[..., half:], values[..., :half]], axis=-1)
    return values * cosine + rolled * sine


def pick_small(table, index):
    match = jnp.arange(table.shape[0], dtype=jnp.int32)[None, :] == index[:, None]
    return jnp.sum(jnp.where(match, table[None, :], 0), axis=1)


def blend(first, second):
    top_one, mass_one, sum_one = first
    top_two, mass_two, sum_two = second
    highest = jnp.maximum(top_one, top_two)
    weight_one = jnp.exp(top_one - highest)
    weight_two = jnp.exp(top_two - highest)
    return (
        highest,
        mass_one * weight_one + mass_two * weight_two,
        sum_one * weight_one[..., None] + sum_two * weight_two[..., None],
    )


def shards(
    hidden_in,
    qkv_weight,
    out_weight,
    q_gain,
    k_gain,
    post_gain,
    final_gain,
    head_weight,
    pool_keys,
    pool_values,
    page_table,
    deal,
    prompt_len,
    segment_ids,
    targets,
    owners,
):
    groups = lax.axis_size("group")
    vocab_count = lax.axis_size("vocab")
    group_idx = lax.axis_index("group")
    vocab_idx = lax.axis_index("vocab")
    head_size = D // HEADS
    heads_dev = HEADS // vocab_count
    score_scale = 1.0 / math.sqrt(head_size)
    request_count = deal.shape[0]
    lane = head_size
    parts = qkv_weight.shape[2] // lane
    rows_here = qkv_weight.shape[1]
    qkv_local = jnp.transpose(qkv_weight.reshape(2, rows_here, parts, lane), (0, 2, 1, 3))
    both_weights = lax.all_gather(
        jnp.concatenate(
            (qkv_local.reshape(2, parts * rows_here, lane), out_weight.reshape(2, -1, lane)), axis=1
        ),
        "group",
    )
    qkv_rows = both_weights[:, :, : parts * rows_here].reshape(groups, 2, parts, rows_here, lane)
    out_rows = both_weights[:, :, parts * rows_here :].reshape((groups,) + out_weight.shape)
    united = jnp.einsum(
        "mtgr,gmjrl->mtjl",
        hidden_in.reshape(2, TOK_G, groups, rows_here),
        qkv_rows,
        preferred_element_type=jnp.float32,
    )
    united = united.reshape(2, TOK_G, heads_dev, 3, head_size)
    query_raw = united[:, :, :, 0, :].reshape(2, TOK_G, heads_dev * head_size)
    key_raw = united[:, :, :, 1, :].reshape(2, TOK_G, heads_dev * head_size)
    squares = lax.all_gather(
        jnp.stack((jnp.sum(query_raw * query_raw, axis=-1), jnp.sum(key_raw * key_raw, axis=-1))),
        "vocab",
    )
    query_sq = jnp.sum(squares[:, 0], axis=0)
    key_sq = jnp.sum(squares[:, 1], axis=0)
    query_normed = query_raw * lax.rsqrt(query_sq[..., None] / D + EPS) * q_gain[:, None, :]
    key_normed = key_raw * lax.rsqrt(key_sq[..., None] / D + EPS) * k_gain[:, None, :]
    seg_ids = lax.dynamic_index_in_dim(segment_ids, group_idx, 0, keepdims=False)
    requests = lax.dynamic_slice_in_dim(deal, group_idx * SEQ_G, SEQ_G)
    seq_numbers = jnp.arange(SEQ_G, dtype=jnp.int32)
    token_index = jnp.arange(TOK_G, dtype=jnp.int32)
    onehot = seg_ids[:, None] == seq_numbers[None, :]
    starts = jnp.sum((seg_ids[None, :] < seq_numbers[:, None]).astype(jnp.int32), axis=1)
    prompt_rows = pick_small(prompt_len, requests)
    tok_start = jnp.sum(jnp.where(onehot, starts[None, :], 0), axis=1)
    tok_prompt = jnp.sum(jnp.where(onehot, prompt_rows[None, :], 0), axis=1)
    positions = (tok_prompt + token_index - tok_start).astype(jnp.float32)
    queries = rotate(query_normed.reshape(2, TOK_G, heads_dev, head_size), positions).astype(
        jnp.bfloat16
    )
    new_keys = rotate(key_normed.reshape(2, TOK_G, heads_dev, head_size), positions).astype(
        jnp.bfloat16
    )
    new_values = united[:, :, :, 2, :].astype(jnp.bfloat16)
    pages_here = pool_keys.shape[1]
    dealt = jnp.take(page_table, deal, axis=0).reshape(groups, SEQ_G, PPG, groups)
    local_pages = (
        lax.dynamic_index_in_dim(dealt, group_idx, 3, keepdims=False) - group_idx * pages_here
    )
    order = jnp.transpose(local_pages, (1, 2, 0))
    send_keys = jnp.take(pool_keys, order, axis=1)
    send_values = jnp.take(pool_values, order, axis=1)
    got_keys, got_values = (
        lax.all_to_all(send_keys, "group", split_axis=3, concat_axis=3, tiled=True),
        lax.all_to_all(send_values, "group", split_axis=3, concat_axis=3, tiled=True),
    )
    cache_rows = got_keys.shape[2] * got_keys.shape[3] * got_keys.shape[4]
    cache_keys = got_keys.reshape(2, SEQ_G, cache_rows, heads_dev, head_size)
    cache_values = got_values.reshape(2, SEQ_G, cache_rows, heads_dev, head_size).astype(
        jnp.float32
    )
    valid = jnp.arange(cache_rows, dtype=jnp.int32)[None, :] < prompt_rows[:, None]
    cache_mask = (onehot[:, :, None] & valid[None, :, :])[None, :, None, :, :]
    cache_scores = (
        jnp.einsum("mthd,mslhd->mthsl", queries, cache_keys, preferred_element_type=jnp.float32)
        * score_scale
    )
    cache_scores = jnp.where(cache_mask, cache_scores, MASKED)
    peak_cache = jnp.max(cache_scores, axis=(3, 4))
    cache_weights = jnp.where(cache_mask, jnp.exp(cache_scores - peak_cache[..., None, None]), 0.0)
    mass_cache = jnp.sum(cache_weights, axis=(3, 4))
    sum_cache = jnp.einsum("mthsl,mslhd->mthd", cache_weights, cache_values)
    same_seq = (seg_ids[:, None] == seg_ids[None, :]) & (
        token_index[None, :] <= token_index[:, None]
    )
    self_mask = same_seq[None, :, None, :]
    self_scores = (
        jnp.einsum("mthd,muhd->mthu", queries, new_keys, preferred_element_type=jnp.float32)
        * score_scale
    )
    self_scores = jnp.where(self_mask, self_scores, MASKED)
    peak_self = jnp.max(self_scores, axis=3)
    self_weights = jnp.where(self_mask, jnp.exp(self_scores - peak_self[..., None]), 0.0)
    mass_self = jnp.sum(self_weights, axis=3)
    sum_self = jnp.einsum("mthu,muhd->mthd", self_weights, new_values.astype(jnp.float32))
    peak_both, mass_both, sum_both = blend(
        (peak_cache, mass_cache, sum_cache), (peak_self, mass_self, sum_self)
    )
    attended = (
        (sum_both / mass_both[..., None])
        .reshape(2, TOK_G, heads_dev * head_size)
        .astype(jnp.bfloat16)
    )
    col_width = D // vocab_count
    pair = groups // vocab_count
    head_rows = jnp.transpose(
        out_rows.reshape((vocab_count, pair) + out_weight.shape), (0, 2, 3, 1, 4)
    ).reshape(vocab_count, 2, heads_dev * head_size, col_width)
    column_block = lax.all_to_all(head_rows, "vocab", split_axis=0, concat_axis=0, tiled=True)
    column_block = jnp.transpose(column_block, (1, 0, 2, 3)).reshape(2, D, col_width)
    attended_all = lax.all_gather(attended, "vocab", axis=2, tiled=True)
    mixed_block = jnp.einsum(
        "mtc,mcd->mtd", attended_all, column_block, preferred_element_type=jnp.float32
    )
    mixed = lax.all_gather(mixed_block.astype(jnp.bfloat16), "vocab", axis=2, tiled=True).astype(
        jnp.float32
    )
    hidden_new = (hidden_in.astype(jnp.float32) + rms_scale(mixed, post_gain[:, None, :])).astype(
        jnp.bfloat16
    )
    hidden_out = lax.dynamic_slice_in_dim(hidden_new, vocab_idx * col_width, col_width, 2)
    final = rms_scale(hidden_new.astype(jnp.float32), final_gain[:, None, :]).astype(jnp.bfloat16)
    voc_here = head_weight.shape[2]
    first_column = (group_idx * vocab_count + vocab_idx) * voc_here
    logits = jnp.einsum(
        "mtd,mdv->mtv",
        lax.all_gather(final, "group", axis=1, tiled=True),
        head_weight,
        preferred_element_type=jnp.float32,
    )
    highest = jnp.max(logits, axis=-1)
    exp_sum = jnp.sum(jnp.exp(logits - highest[..., None]), axis=-1)
    wanted = targets - first_column
    found = jnp.arange(voc_here, dtype=jnp.int32)[None, :] == wanted[:, None]
    picked = jnp.sum(jnp.where(found[None], logits, 0.0), axis=-1)
    slot_numbers = jnp.arange(request_count, dtype=jnp.int32)
    request_of_slot = jnp.sum(
        jnp.where(owners[None, :] == slot_numbers[:, None], slot_numbers[None, :], 0), axis=1
    )
    place_of_slot = jnp.sum(
        jnp.where(deal[None, :] == request_of_slot[:, None], slot_numbers[None, :], 0), axis=1
    )
    group_of_slot = place_of_slot // SEQ_G
    seq_of_slot = place_of_slot % SEQ_G
    dest_groups = jnp.arange(groups, dtype=jnp.int32)
    slots_per_group = request_count // groups
    row_groups = jnp.concatenate(
        (dest_groups[:, None], group_of_slot.reshape(groups, slots_per_group)), axis=1
    )
    statistics = jnp.stack((highest, exp_sum, picked), axis=0).reshape(3, 2, groups, TOK_G)
    rows = jnp.take(statistics, row_groups.reshape(-1), axis=2).reshape(
        3, 2, groups, 1 + slots_per_group, TOK_G
    )
    rows = jnp.transpose(rows, (2, 3, 0, 1, 4))
    got = lax.all_to_all(rows, "group", split_axis=0, concat_axis=0, tiled=True)
    peak_one = jnp.max(got[:, :, 0], axis=0)
    mass_one = jnp.sum(got[:, :, 1] * jnp.exp(got[:, :, 0] - peak_one[None]), axis=0)
    target_one = jnp.sum(got[:, :, 2], axis=0)
    gathered = lax.all_gather(jnp.stack((peak_one, mass_one, target_one), axis=0), "vocab")
    peak_logit = jnp.max(gathered[:, 0], axis=0)
    exp_total = jnp.sum(gathered[:, 1] * jnp.exp(gathered[:, 0] - peak_logit[None]), axis=0)
    target_logit = jnp.sum(gathered[:, 2], axis=0)
    logprobs = target_logit - (peak_logit + jnp.log(exp_total))
    own_logprobs = logprobs[0]
    my_slots = group_idx * slots_per_group + jnp.arange(slots_per_group, dtype=jnp.int32)
    slot_groups = jnp.take(group_of_slot, my_slots)
    slot_seqs = jnp.take(seq_of_slot, my_slots)
    slot_ids = jnp.take(segment_ids, slot_groups, axis=0)
    in_seq = (slot_ids == slot_seqs[:, None]).astype(jnp.float32)
    slot_gap = logprobs[1:, 0] - logprobs[1:, 1]
    seq_diff = jnp.sum(in_seq * slot_gap, axis=1) / jnp.sum(in_seq, axis=1)
    return (hidden_out, own_logprobs, seq_diff)


def solution(mesh):
    return jax.shard_map(
        shards,
        mesh=mesh,
        in_specs=(
            P(None, "group", None),
            P(None, "group", "vocab"),
            P(None, "vocab", "group"),
            P(None, "vocab"),
            P(None, "vocab"),
            P(),
            P(),
            P(None, None, ("group", "vocab")),
            P(None, "group", None, "vocab"),
            P(None, "group", None, "vocab"),
            P(),
            P(),
            P(),
            P(),
            P(),
            P(),
        ),
        out_specs=(P(None, "group", "vocab"), P(None, "group"), P("group")),
        check_vma=False,
    )
```

```python
import math

import jax
import jax.numpy as jnp
from jax import lax
from jax.sharding import PartitionSpec as P

D = 2048
HEADS = 16
TOK_G = 64
SEQ_G = 2
PPG = 1


EPS = 1e-06
THETA = 500000.0
MASKED = -1e30


def rms_scale(values, gain):
    mean_sq = jnp.mean(values * values, axis=-1, keepdims=True)
    return values * lax.rsqrt(mean_sq + EPS) * gain


def rotate(values, positions):
    half = values.shape[-1] // 2
    freq = THETA ** (-(jnp.arange(half, dtype=jnp.float32) * 2.0 / values.shape[-1]))
    angle = positions[:, None] * freq[None, :]
    cosine = jnp.concatenate([jnp.cos(angle), jnp.cos(angle)], axis=-1)[:, None, :]
    sine = jnp.concatenate([jnp.sin(angle), jnp.sin(angle)], axis=-1)[:, None, :]
    rolled = jnp.concatenate([-values[..., half:], values[..., :half]], axis=-1)
    return values * cosine + rolled * sine


def pick_small(table, index):
    match = jnp.arange(table.shape[0], dtype=jnp.int32)[None, :] == index[:, None]
    return jnp.sum(jnp.where(match, table[None, :], 0), axis=1)


def blend(first, second):
    top_one, mass_one, sum_one = first
    top_two, mass_two, sum_two = second
    highest = jnp.maximum(top_one, top_two)
    weight_one = jnp.exp(top_one - highest)
    weight_two = jnp.exp(top_two - highest)
    return (
        highest,
        mass_one * weight_one + mass_two * weight_two,
        sum_one * weight_one[..., None] + sum_two * weight_two[..., None],
    )


def shards(
    hidden_in,
    qkv_weight,
    out_weight,
    q_gain,
    k_gain,
    post_gain,
    final_gain,
    head_weight,
    pool_keys,
    pool_values,
    page_table,
    deal,
    prompt_len,
    segment_ids,
    targets,
    owners,
):
    groups = lax.axis_size("group")
    vocab_count = lax.axis_size("vocab")
    group_idx = lax.axis_index("group")
    vocab_idx = lax.axis_index("vocab")
    head_size = D // HEADS
    heads_dev = HEADS // vocab_count
    score_scale = 1.0 / math.sqrt(head_size)
    request_count = deal.shape[0]
    lane = head_size
    parts = qkv_weight.shape[2] // lane
    rows_here = qkv_weight.shape[1]
    qkv_local = jnp.transpose(qkv_weight.reshape(2, rows_here, parts, lane), (0, 2, 1, 3))
    both_weights = lax.all_gather(
        jnp.concatenate(
            (qkv_local.reshape(2, parts * rows_here, lane), out_weight.reshape(2, -1, lane)), axis=1
        ),
        "group",
    )
    qkv_rows = both_weights[:, :, : parts * rows_here].reshape(groups, 2, parts, rows_here, lane)
    out_rows = both_weights[:, :, parts * rows_here :].reshape((groups,) + out_weight.shape)
    united = jnp.einsum(
        "mtgr,gmjrl->mtjl",
        hidden_in.reshape(2, TOK_G, groups, rows_here),
        qkv_rows,
        preferred_element_type=jnp.float32,
    )
    united = united.reshape(2, TOK_G, heads_dev, 3, head_size)
    query_raw = united[:, :, :, 0, :].reshape(2, TOK_G, heads_dev * head_size)
    key_raw = united[:, :, :, 1, :].reshape(2, TOK_G, heads_dev * head_size)
    squares = lax.all_gather(
        jnp.stack((jnp.sum(query_raw * query_raw, axis=-1), jnp.sum(key_raw * key_raw, axis=-1))),
        "vocab",
    )
    query_sq = jnp.sum(squares[:, 0], axis=0)
    key_sq = jnp.sum(squares[:, 1], axis=0)
    query_normed = query_raw * lax.rsqrt(query_sq[..., None] / D + EPS) * q_gain[:, None, :]
    key_normed = key_raw * lax.rsqrt(key_sq[..., None] / D + EPS) * k_gain[:, None, :]
    seg_ids = lax.dynamic_index_in_dim(segment_ids, group_idx, 0, keepdims=False)
    requests = lax.dynamic_slice_in_dim(deal, group_idx * SEQ_G, SEQ_G)
    seq_numbers = jnp.arange(SEQ_G, dtype=jnp.int32)
    token_index = jnp.arange(TOK_G, dtype=jnp.int32)
    onehot = seg_ids[:, None] == seq_numbers[None, :]
    starts = jnp.sum((seg_ids[None, :] < seq_numbers[:, None]).astype(jnp.int32), axis=1)
    prompt_rows = pick_small(prompt_len, requests)
    tok_start = jnp.sum(jnp.where(onehot, starts[None, :], 0), axis=1)
    tok_prompt = jnp.sum(jnp.where(onehot, prompt_rows[None, :], 0), axis=1)
    positions = (tok_prompt + token_index - tok_start).astype(jnp.float32)
    queries = rotate(query_normed.reshape(2, TOK_G, heads_dev, head_size), positions).astype(
        jnp.bfloat16
    )
    new_keys = rotate(key_normed.reshape(2, TOK_G, heads_dev, head_size), positions).astype(
        jnp.bfloat16
    )
    new_values = united[:, :, :, 2, :].astype(jnp.bfloat16)
    pages_here = pool_keys.shape[1]
    dealt = jnp.take(page_table, deal, axis=0).reshape(groups, SEQ_G, PPG, groups)
    local_pages = (
        lax.dynamic_index_in_dim(dealt, group_idx, 3, keepdims=False) - group_idx * pages_here
    )
    order = jnp.transpose(local_pages, (1, 2, 0))
    send_keys = jnp.take(pool_keys, order, axis=1)
    send_values = jnp.take(pool_values, order, axis=1)
    got_pages = lax.all_to_all(
        jnp.stack((send_keys, send_values)), "group", split_axis=4, concat_axis=4, tiled=True
    )
    got_keys, got_values = got_pages[0], got_pages[1]
    cache_rows = got_keys.shape[2] * got_keys.shape[3] * got_keys.shape[4]
    cache_keys = got_keys.reshape(2, SEQ_G, cache_rows, heads_dev, head_size)
    cache_values = got_values.reshape(2, SEQ_G, cache_rows, heads_dev, head_size).astype(
        jnp.float32
    )
    valid = jnp.arange(cache_rows, dtype=jnp.int32)[None, :] < prompt_rows[:, None]
    cache_mask = (onehot[:, :, None] & valid[None, :, :])[None, :, None, :, :]
    cache_scores = (
        jnp.einsum("mthd,mslhd->mthsl", queries, cache_keys, preferred_element_type=jnp.float32)
        * score_scale
    )
    cache_scores = jnp.where(cache_mask, cache_scores, MASKED)
    peak_cache = jnp.max(cache_scores, axis=(3, 4))
    cache_weights = jnp.where(cache_mask, jnp.exp(cache_scores - peak_cache[..., None, None]), 0.0)
    mass_cache = jnp.sum(cache_weights, axis=(3, 4))
    sum_cache = jnp.einsum("mthsl,mslhd->mthd", cache_weights, cache_values)
    same_seq = (seg_ids[:, None] == seg_ids[None, :]) & (
        token_index[None, :] <= token_index[:, None]
    )
    self_mask = same_seq[None, :, None, :]
    self_scores = (
        jnp.einsum("mthd,muhd->mthu", queries, new_keys, preferred_element_type=jnp.float32)
        * score_scale
    )
    self_scores = jnp.where(self_mask, self_scores, MASKED)
    peak_self = jnp.max(self_scores, axis=3)
    self_weights = jnp.where(self_mask, jnp.exp(self_scores - peak_self[..., None]), 0.0)
    mass_self = jnp.sum(self_weights, axis=3)
    sum_self = jnp.einsum("mthu,muhd->mthd", self_weights, new_values.astype(jnp.float32))
    peak_both, mass_both, sum_both = blend(
        (peak_cache, mass_cache, sum_cache), (peak_self, mass_self, sum_self)
    )
    attended = (
        (sum_both / mass_both[..., None])
        .reshape(2, TOK_G, heads_dev * head_size)
        .astype(jnp.bfloat16)
    )
    col_width = D // vocab_count
    pair = groups // vocab_count
    head_rows = jnp.transpose(
        out_rows.reshape((vocab_count, pair) + out_weight.shape), (0, 2, 3, 1, 4)
    ).reshape(vocab_count, 2, heads_dev * head_size, col_width)
    column_block = lax.all_to_all(head_rows, "vocab", split_axis=0, concat_axis=0, tiled=True)
    column_block = jnp.transpose(column_block, (1, 0, 2, 3)).reshape(2, D, col_width)
    attended_all = lax.all_gather(attended, "vocab", axis=2, tiled=True)
    mixed_block = jnp.einsum(
        "mtc,mcd->mtd", attended_all, column_block, preferred_element_type=jnp.float32
    )
    mixed = lax.all_gather(mixed_block.astype(jnp.bfloat16), "vocab", axis=2, tiled=True).astype(
        jnp.float32
    )
    hidden_new = (hidden_in.astype(jnp.float32) + rms_scale(mixed, post_gain[:, None, :])).astype(
        jnp.bfloat16
    )
    hidden_out = lax.dynamic_slice_in_dim(hidden_new, vocab_idx * col_width, col_width, 2)
    final = rms_scale(hidden_new.astype(jnp.float32), final_gain[:, None, :]).astype(jnp.bfloat16)
    voc_here = head_weight.shape[2]
    first_column = (group_idx * vocab_count + vocab_idx) * voc_here
    logits = jnp.einsum(
        "mtd,mdv->mtv",
        lax.all_gather(final, "group", axis=1, tiled=True),
        head_weight,
        preferred_element_type=jnp.float32,
    )
    highest = jnp.max(logits, axis=-1)
    exp_sum = jnp.sum(jnp.exp(logits - highest[..., None]), axis=-1)
    wanted = targets - first_column
    found = jnp.arange(voc_here, dtype=jnp.int32)[None, :] == wanted[:, None]
    picked = jnp.sum(jnp.where(found[None], logits, 0.0), axis=-1)
    slot_numbers = jnp.arange(request_count, dtype=jnp.int32)
    request_of_slot = jnp.sum(
        jnp.where(owners[None, :] == slot_numbers[:, None], slot_numbers[None, :], 0), axis=1
    )
    place_of_slot = jnp.sum(
        jnp.where(deal[None, :] == request_of_slot[:, None], slot_numbers[None, :], 0), axis=1
    )
    group_of_slot = place_of_slot // SEQ_G
    seq_of_slot = place_of_slot % SEQ_G
    dest_groups = jnp.arange(groups, dtype=jnp.int32)
    slots_per_group = request_count // groups
    row_groups = jnp.concatenate(
        (dest_groups[:, None], group_of_slot.reshape(groups, slots_per_group)), axis=1
    )
    statistics = jnp.stack((highest, exp_sum, picked), axis=0).reshape(3, 2, groups, TOK_G)
    rows = jnp.take(statistics, row_groups.reshape(-1), axis=2).reshape(
        3, 2, groups, 1 + slots_per_group, TOK_G
    )
    rows = jnp.transpose(rows, (2, 3, 0, 1, 4))
    got = lax.all_to_all(rows, "group", split_axis=0, concat_axis=0, tiled=True)
    peak_one = jnp.max(got[:, :, 0], axis=0)
    mass_one = jnp.sum(got[:, :, 1] * jnp.exp(got[:, :, 0] - peak_one[None]), axis=0)
    target_one = jnp.sum(got[:, :, 2], axis=0)
    gathered = lax.all_gather(jnp.stack((peak_one, mass_one, target_one), axis=0), "vocab")
    peak_logit = jnp.max(gathered[:, 0], axis=0)
    exp_total = jnp.sum(gathered[:, 1] * jnp.exp(gathered[:, 0] - peak_logit[None]), axis=0)
    target_logit = jnp.sum(gathered[:, 2], axis=0)
    logprobs = target_logit - (peak_logit + jnp.log(exp_total))
    own_logprobs = logprobs[0]
    my_slots = group_idx * slots_per_group + jnp.arange(slots_per_group, dtype=jnp.int32)
    slot_groups = jnp.take(group_of_slot, my_slots)
    slot_seqs = jnp.take(seq_of_slot, my_slots)
    slot_ids = jnp.take(segment_ids, slot_groups, axis=0)
    in_seq = (slot_ids == slot_seqs[:, None]).astype(jnp.float32)
    slot_gap = logprobs[1:, 0] - logprobs[1:, 1]
    seq_diff = jnp.sum(in_seq * slot_gap, axis=1) / jnp.sum(in_seq, axis=1)
    return (hidden_out, own_logprobs, seq_diff)


def solution(mesh):
    return jax.shard_map(
        shards,
        mesh=mesh,
        in_specs=(
            P(None, "group", None),
            P(None, "group", "vocab"),
            P(None, "vocab", "group"),
            P(None, "vocab"),
            P(None, "vocab"),
            P(),
            P(),
            P(None, None, ("group", "vocab")),
            P(None, "group", None, "vocab"),
            P(None, "group", None, "vocab"),
            P(),
            P(),
            P(),
            P(),
            P(),
            P(),
        ),
        out_specs=(P(None, "group", "vocab"), P(None, "group"), P("group")),
        check_vma=False,
    )
```

```python
import math

import jax
import jax.numpy as jnp
from jax import lax
from jax.sharding import PartitionSpec as P

D = 2048
HEADS = 16
TOK_G = 64
SEQ_G = 2
PPG = 1


EPS = 1e-06
THETA = 500000.0
MASKED = -1e30


def rms_scale(values, gain):
    mean_sq = jnp.mean(values * values, axis=-1, keepdims=True)
    return values * lax.rsqrt(mean_sq + EPS) * gain


def rotate(values, positions):
    half = values.shape[-1] // 2
    freq = THETA ** (-(jnp.arange(half, dtype=jnp.float32) * 2.0 / values.shape[-1]))
    angle = positions[:, None] * freq[None, :]
    cosine = jnp.concatenate([jnp.cos(angle), jnp.cos(angle)], axis=-1)[:, None, :]
    sine = jnp.concatenate([jnp.sin(angle), jnp.sin(angle)], axis=-1)[:, None, :]
    rolled = jnp.concatenate([-values[..., half:], values[..., :half]], axis=-1)
    return values * cosine + rolled * sine


def pick_small(table, index):
    match = jnp.arange(table.shape[0], dtype=jnp.int32)[None, :] == index[:, None]
    return jnp.sum(jnp.where(match, table[None, :], 0), axis=1)


def blend(first, second):
    top_one, mass_one, sum_one = first
    top_two, mass_two, sum_two = second
    highest = jnp.maximum(top_one, top_two)
    weight_one = jnp.exp(top_one - highest)
    weight_two = jnp.exp(top_two - highest)
    return (
        highest,
        mass_one * weight_one + mass_two * weight_two,
        sum_one * weight_one[..., None] + sum_two * weight_two[..., None],
    )


def shards(
    hidden_in,
    qkv_weight,
    out_weight,
    q_gain,
    k_gain,
    post_gain,
    final_gain,
    head_weight,
    pool_keys,
    pool_values,
    page_table,
    deal,
    prompt_len,
    segment_ids,
    targets,
    owners,
):
    groups = lax.axis_size("group")
    vocab_count = lax.axis_size("vocab")
    group_idx = lax.axis_index("group")
    vocab_idx = lax.axis_index("vocab")
    head_size = D // HEADS
    heads_dev = HEADS // vocab_count
    score_scale = 1.0 / math.sqrt(head_size)
    request_count = deal.shape[0]
    lane = head_size
    parts = qkv_weight.shape[2] // lane
    rows_here = qkv_weight.shape[1]
    qkv_local = jnp.transpose(qkv_weight.reshape(2, rows_here, parts, lane), (0, 2, 1, 3))
    both_weights = jnp.concatenate(
        (qkv_local.reshape(2, parts * rows_here, lane), out_weight.reshape(2, -1, lane)), axis=1
    )[None]
    step = 1
    while step < groups:
        other = lax.ppermute(both_weights, "group", [(i, i ^ step) for i in range(groups)])
        both_weights = jnp.where(
            (group_idx // step) % 2 == 0,
            jnp.concatenate((both_weights, other)),
            jnp.concatenate((other, both_weights)),
        )
        step *= 2
    qkv_rows = both_weights[:, :, : parts * rows_here].reshape(groups, 2, parts, rows_here, lane)
    out_rows = both_weights[:, :, parts * rows_here :].reshape((groups,) + out_weight.shape)
    united = jnp.einsum(
        "mtgr,gmjrl->mtjl",
        hidden_in.reshape(2, TOK_G, groups, rows_here),
        qkv_rows,
        preferred_element_type=jnp.float32,
    )
    united = united.reshape(2, TOK_G, heads_dev, 3, head_size)
    query_raw = united[:, :, :, 0, :].reshape(2, TOK_G, heads_dev * head_size)
    key_raw = united[:, :, :, 1, :].reshape(2, TOK_G, heads_dev * head_size)
    squares = lax.all_gather(
        jnp.stack((jnp.sum(query_raw * query_raw, axis=-1), jnp.sum(key_raw * key_raw, axis=-1))),
        "vocab",
    )
    query_sq = jnp.sum(squares[:, 0], axis=0)
    key_sq = jnp.sum(squares[:, 1], axis=0)
    query_normed = query_raw * lax.rsqrt(query_sq[..., None] / D + EPS) * q_gain[:, None, :]
    key_normed = key_raw * lax.rsqrt(key_sq[..., None] / D + EPS) * k_gain[:, None, :]
    seg_ids = lax.dynamic_index_in_dim(segment_ids, group_idx, 0, keepdims=False)
    requests = lax.dynamic_slice_in_dim(deal, group_idx * SEQ_G, SEQ_G)
    seq_numbers = jnp.arange(SEQ_G, dtype=jnp.int32)
    token_index = jnp.arange(TOK_G, dtype=jnp.int32)
    onehot = seg_ids[:, None] == seq_numbers[None, :]
    starts = jnp.sum((seg_ids[None, :] < seq_numbers[:, None]).astype(jnp.int32), axis=1)
    prompt_rows = pick_small(prompt_len, requests)
    tok_start = jnp.sum(jnp.where(onehot, starts[None, :], 0), axis=1)
    tok_prompt = jnp.sum(jnp.where(onehot, prompt_rows[None, :], 0), axis=1)
    positions = (tok_prompt + token_index - tok_start).astype(jnp.float32)
    queries = rotate(query_normed.reshape(2, TOK_G, heads_dev, head_size), positions).astype(
        jnp.bfloat16
    )
    new_keys = rotate(key_normed.reshape(2, TOK_G, heads_dev, head_size), positions).astype(
        jnp.bfloat16
    )
    new_values = united[:, :, :, 2, :].astype(jnp.bfloat16)
    pages_here = pool_keys.shape[1]
    dealt = jnp.take(page_table, deal, axis=0).reshape(groups, SEQ_G, PPG, groups)
    local_pages = (
        lax.dynamic_index_in_dim(dealt, group_idx, 3, keepdims=False) - group_idx * pages_here
    )
    order = jnp.transpose(local_pages, (1, 2, 0))
    send_keys = jnp.take(pool_keys, order, axis=1)
    send_values = jnp.take(pool_values, order, axis=1)
    got_pages = lax.all_to_all(
        jnp.stack((send_keys, send_values)), "group", split_axis=4, concat_axis=4, tiled=True
    )
    got_keys, got_values = got_pages[0], got_pages[1]
    cache_rows = got_keys.shape[2] * got_keys.shape[3] * got_keys.shape[4]
    cache_keys = got_keys.reshape(2, SEQ_G, cache_rows, heads_dev, head_size)
    cache_values = got_values.reshape(2, SEQ_G, cache_rows, heads_dev, head_size).astype(
        jnp.float32
    )
    valid = jnp.arange(cache_rows, dtype=jnp.int32)[None, :] < prompt_rows[:, None]
    cache_mask = (onehot[:, :, None] & valid[None, :, :])[None, :, None, :, :]
    cache_scores = (
        jnp.einsum("mthd,mslhd->mthsl", queries, cache_keys, preferred_element_type=jnp.float32)
        * score_scale
    )
    cache_scores = jnp.where(cache_mask, cache_scores, MASKED)
    peak_cache = jnp.max(cache_scores, axis=(3, 4))
    cache_weights = jnp.where(cache_mask, jnp.exp(cache_scores - peak_cache[..., None, None]), 0.0)
    mass_cache = jnp.sum(cache_weights, axis=(3, 4))
    sum_cache = jnp.einsum("mthsl,mslhd->mthd", cache_weights, cache_values)
    same_seq = (seg_ids[:, None] == seg_ids[None, :]) & (
        token_index[None, :] <= token_index[:, None]
    )
    self_mask = same_seq[None, :, None, :]
    self_scores = (
        jnp.einsum("mthd,muhd->mthu", queries, new_keys, preferred_element_type=jnp.float32)
        * score_scale
    )
    self_scores = jnp.where(self_mask, self_scores, MASKED)
    peak_self = jnp.max(self_scores, axis=3)
    self_weights = jnp.where(self_mask, jnp.exp(self_scores - peak_self[..., None]), 0.0)
    mass_self = jnp.sum(self_weights, axis=3)
    sum_self = jnp.einsum("mthu,muhd->mthd", self_weights, new_values.astype(jnp.float32))
    peak_both, mass_both, sum_both = blend(
        (peak_cache, mass_cache, sum_cache), (peak_self, mass_self, sum_self)
    )
    attended = (
        (sum_both / mass_both[..., None])
        .reshape(2, TOK_G, heads_dev * head_size)
        .astype(jnp.bfloat16)
    )
    col_width = D // vocab_count
    pair = groups // vocab_count
    head_rows = jnp.transpose(
        out_rows.reshape((vocab_count, pair) + out_weight.shape), (0, 2, 3, 1, 4)
    ).reshape(vocab_count, 2, heads_dev * head_size, col_width)
    column_block = lax.all_to_all(head_rows, "vocab", split_axis=0, concat_axis=0, tiled=True)
    column_block = jnp.transpose(column_block, (1, 0, 2, 3)).reshape(2, D, col_width)
    attended_all = lax.all_gather(attended, "vocab", axis=2, tiled=True)
    mixed_block = jnp.einsum(
        "mtc,mcd->mtd", attended_all, column_block, preferred_element_type=jnp.float32
    )
    mixed = lax.all_gather(mixed_block.astype(jnp.bfloat16), "vocab", axis=2, tiled=True).astype(
        jnp.float32
    )
    hidden_new = (hidden_in.astype(jnp.float32) + rms_scale(mixed, post_gain[:, None, :])).astype(
        jnp.bfloat16
    )
    hidden_out = lax.dynamic_slice_in_dim(hidden_new, vocab_idx * col_width, col_width, 2)
    final = rms_scale(hidden_new.astype(jnp.float32), final_gain[:, None, :]).astype(jnp.bfloat16)
    voc_here = head_weight.shape[2]
    first_column = (group_idx * vocab_count + vocab_idx) * voc_here
    logits = jnp.einsum(
        "mtd,mdv->mtv",
        lax.all_gather(final, "group", axis=1, tiled=True),
        head_weight,
        preferred_element_type=jnp.float32,
    )
    highest = jnp.max(logits, axis=-1)
    exp_sum = jnp.sum(jnp.exp(logits - highest[..., None]), axis=-1)
    wanted = targets - first_column
    found = jnp.arange(voc_here, dtype=jnp.int32)[None, :] == wanted[:, None]
    picked = jnp.sum(jnp.where(found[None], logits, 0.0), axis=-1)
    slot_numbers = jnp.arange(request_count, dtype=jnp.int32)
    request_of_slot = jnp.sum(
        jnp.where(owners[None, :] == slot_numbers[:, None], slot_numbers[None, :], 0), axis=1
    )
    place_of_slot = jnp.sum(
        jnp.where(deal[None, :] == request_of_slot[:, None], slot_numbers[None, :], 0), axis=1
    )
    group_of_slot = place_of_slot // SEQ_G
    seq_of_slot = place_of_slot % SEQ_G
    dest_groups = jnp.arange(groups, dtype=jnp.int32)
    slots_per_group = request_count // groups
    row_groups = jnp.concatenate(
        (dest_groups[:, None], group_of_slot.reshape(groups, slots_per_group)), axis=1
    )
    statistics = jnp.stack((highest, exp_sum, picked), axis=0).reshape(3, 2, groups, TOK_G)
    rows = jnp.take(statistics, row_groups.reshape(-1), axis=2).reshape(
        3, 2, groups, 1 + slots_per_group, TOK_G
    )
    rows = jnp.transpose(rows, (2, 3, 0, 1, 4))
    got = lax.all_to_all(rows, "group", split_axis=0, concat_axis=0, tiled=True)
    peak_one = jnp.max(got[:, :, 0], axis=0)
    mass_one = jnp.sum(got[:, :, 1] * jnp.exp(got[:, :, 0] - peak_one[None]), axis=0)
    target_one = jnp.sum(got[:, :, 2], axis=0)
    gathered = lax.all_gather(jnp.stack((peak_one, mass_one, target_one), axis=0), "vocab")
    peak_logit = jnp.max(gathered[:, 0], axis=0)
    exp_total = jnp.sum(gathered[:, 1] * jnp.exp(gathered[:, 0] - peak_logit[None]), axis=0)
    target_logit = jnp.sum(gathered[:, 2], axis=0)
    logprobs = target_logit - (peak_logit + jnp.log(exp_total))
    own_logprobs = logprobs[0]
    my_slots = group_idx * slots_per_group + jnp.arange(slots_per_group, dtype=jnp.int32)
    slot_groups = jnp.take(group_of_slot, my_slots)
    slot_seqs = jnp.take(seq_of_slot, my_slots)
    slot_ids = jnp.take(segment_ids, slot_groups, axis=0)
    in_seq = (slot_ids == slot_seqs[:, None]).astype(jnp.float32)
    slot_gap = logprobs[1:, 0] - logprobs[1:, 1]
    seq_diff = jnp.sum(in_seq * slot_gap, axis=1) / jnp.sum(in_seq, axis=1)
    return (hidden_out, own_logprobs, seq_diff)


def solution(mesh):
    return jax.shard_map(
        shards,
        mesh=mesh,
        in_specs=(
            P(None, "group", None),
            P(None, "group", "vocab"),
            P(None, "vocab", "group"),
            P(None, "vocab"),
            P(None, "vocab"),
            P(),
            P(),
            P(None, None, ("group", "vocab")),
            P(None, "group", None, "vocab"),
            P(None, "group", None, "vocab"),
            P(),
            P(),
            P(),
            P(),
            P(),
            P(),
        ),
        out_specs=(P(None, "group", "vocab"), P(None, "group"), P("group")),
        check_vma=False,
    )
```

```python
import math

import jax
import jax.numpy as jnp
from jax import lax
from jax.sharding import PartitionSpec as P

D = 2048
HEADS = 16
TOK_G = 64
SEQ_G = 2
PPG = 1


EPS = 1e-06
THETA = 500000.0
MASKED = -1e30


def rms_scale(values, gain):
    mean_sq = jnp.mean(values * values, axis=-1, keepdims=True)
    return values * lax.rsqrt(mean_sq + EPS) * gain


def rotate(values, positions):
    half = values.shape[-1] // 2
    freq = THETA ** (-(jnp.arange(half, dtype=jnp.float32) * 2.0 / values.shape[-1]))
    angle = positions[:, None] * freq[None, :]
    cosine = jnp.concatenate([jnp.cos(angle), jnp.cos(angle)], axis=-1)[:, None, :]
    sine = jnp.concatenate([jnp.sin(angle), jnp.sin(angle)], axis=-1)[:, None, :]
    rolled = jnp.concatenate([-values[..., half:], values[..., :half]], axis=-1)
    return values * cosine + rolled * sine


def pick_small(table, index):
    match = jnp.arange(table.shape[0], dtype=jnp.int32)[None, :] == index[:, None]
    return jnp.sum(jnp.where(match, table[None, :], 0), axis=1)


def blend(first, second):
    top_one, mass_one, sum_one = first
    top_two, mass_two, sum_two = second
    highest = jnp.maximum(top_one, top_two)
    weight_one = jnp.exp(top_one - highest)
    weight_two = jnp.exp(top_two - highest)
    return (
        highest,
        mass_one * weight_one + mass_two * weight_two,
        sum_one * weight_one[..., None] + sum_two * weight_two[..., None],
    )


def shards(
    hidden_in,
    qkv_weight,
    out_weight,
    q_gain,
    k_gain,
    post_gain,
    final_gain,
    head_weight,
    pool_keys,
    pool_values,
    page_table,
    deal,
    prompt_len,
    segment_ids,
    targets,
    owners,
):
    groups = lax.axis_size("group")
    vocab_count = lax.axis_size("vocab")
    group_idx = lax.axis_index("group")
    vocab_idx = lax.axis_index("vocab")
    head_size = D // HEADS
    heads_dev = HEADS // vocab_count
    score_scale = 1.0 / math.sqrt(head_size)
    request_count = deal.shape[0]
    lane = head_size
    parts = qkv_weight.shape[2] // lane
    rows_here = qkv_weight.shape[1]
    qkv_local = jnp.transpose(qkv_weight.reshape(2, rows_here, parts, lane), (0, 2, 1, 3))
    both_weights = lax.all_gather(
        jnp.concatenate(
            (qkv_local.reshape(2, parts * rows_here, lane), out_weight.reshape(2, -1, lane)), axis=1
        ),
        "group",
    )
    qkv_rows = both_weights[:, :, : parts * rows_here].reshape(groups, 2, parts, rows_here, lane)
    out_rows = both_weights[:, :, parts * rows_here :].reshape((groups,) + out_weight.shape)
    united = jnp.einsum(
        "mtgr,gmjrl->mtjl",
        hidden_in.reshape(2, TOK_G, groups, rows_here),
        qkv_rows,
        preferred_element_type=jnp.float32,
    )
    united = united.reshape(2, TOK_G, heads_dev, 3, head_size)
    query_raw = united[:, :, :, 0, :].reshape(2, TOK_G, heads_dev * head_size)
    key_raw = united[:, :, :, 1, :].reshape(2, TOK_G, heads_dev * head_size)
    squares = lax.all_gather(
        jnp.stack((jnp.sum(query_raw * query_raw, axis=-1), jnp.sum(key_raw * key_raw, axis=-1))),
        "vocab",
    )
    query_sq = jnp.sum(squares[:, 0], axis=0)
    key_sq = jnp.sum(squares[:, 1], axis=0)
    query_normed = query_raw * lax.rsqrt(query_sq[..., None] / D + EPS) * q_gain[:, None, :]
    key_normed = key_raw * lax.rsqrt(key_sq[..., None] / D + EPS) * k_gain[:, None, :]
    seg_ids = lax.dynamic_index_in_dim(segment_ids, group_idx, 0, keepdims=False)
    requests = lax.dynamic_slice_in_dim(deal, group_idx * SEQ_G, SEQ_G)
    seq_numbers = jnp.arange(SEQ_G, dtype=jnp.int32)
    token_index = jnp.arange(TOK_G, dtype=jnp.int32)
    onehot = seg_ids[:, None] == seq_numbers[None, :]
    starts = jnp.sum((seg_ids[None, :] < seq_numbers[:, None]).astype(jnp.int32), axis=1)
    prompt_rows = pick_small(prompt_len, requests)
    tok_start = jnp.sum(jnp.where(onehot, starts[None, :], 0), axis=1)
    tok_prompt = jnp.sum(jnp.where(onehot, prompt_rows[None, :], 0), axis=1)
    positions = (tok_prompt + token_index - tok_start).astype(jnp.float32)
    queries = rotate(query_normed.reshape(2, TOK_G, heads_dev, head_size), positions).astype(
        jnp.bfloat16
    )
    new_keys = rotate(key_normed.reshape(2, TOK_G, heads_dev, head_size), positions).astype(
        jnp.bfloat16
    )
    new_values = united[:, :, :, 2, :].astype(jnp.bfloat16)
    pages_here = pool_keys.shape[1]
    dealt = jnp.take(page_table, deal, axis=0).reshape(groups, SEQ_G, PPG, groups)
    local_pages = (
        lax.dynamic_index_in_dim(dealt, group_idx, 3, keepdims=False) - group_idx * pages_here
    )
    order = jnp.transpose(local_pages, (1, 2, 0))
    send_keys = jnp.take(pool_keys, order, axis=1)
    send_values = jnp.take(pool_values, order, axis=1)
    got_keys, got_values = (
        lax.all_to_all(send_keys, "group", split_axis=3, concat_axis=3, tiled=True),
        lax.all_to_all(send_values, "group", split_axis=3, concat_axis=3, tiled=True),
    )
    cache_rows = got_keys.shape[2] * got_keys.shape[3] * got_keys.shape[4]
    cache_keys = got_keys.reshape(2, SEQ_G, cache_rows, heads_dev, head_size)
    cache_values = got_values.reshape(2, SEQ_G, cache_rows, heads_dev, head_size).astype(
        jnp.float32
    )
    valid = jnp.arange(cache_rows, dtype=jnp.int32)[None, :] < prompt_rows[:, None]
    cache_mask = (onehot[:, :, None] & valid[None, :, :])[None, :, None, :, :]
    cache_scores = (
        jnp.einsum("mthd,mslhd->mthsl", queries, cache_keys, preferred_element_type=jnp.float32)
        * score_scale
    )
    cache_scores = jnp.where(cache_mask, cache_scores, MASKED)
    peak_cache = jnp.max(cache_scores, axis=(3, 4))
    cache_weights = jnp.where(cache_mask, jnp.exp(cache_scores - peak_cache[..., None, None]), 0.0)
    mass_cache = jnp.sum(cache_weights, axis=(3, 4))
    sum_cache = jnp.einsum("mthsl,mslhd->mthd", cache_weights, cache_values)
    same_seq = (seg_ids[:, None] == seg_ids[None, :]) & (
        token_index[None, :] <= token_index[:, None]
    )
    self_mask = same_seq[None, :, None, :]
    self_scores = (
        jnp.einsum("mthd,muhd->mthu", queries, new_keys, preferred_element_type=jnp.float32)
        * score_scale
    )
    self_scores = jnp.where(self_mask, self_scores, MASKED)
    peak_self = jnp.max(self_scores, axis=3)
    self_weights = jnp.where(self_mask, jnp.exp(self_scores - peak_self[..., None]), 0.0)
    mass_self = jnp.sum(self_weights, axis=3)
    sum_self = jnp.einsum("mthu,muhd->mthd", self_weights, new_values.astype(jnp.float32))
    peak_both, mass_both, sum_both = blend(
        (peak_cache, mass_cache, sum_cache), (peak_self, mass_self, sum_self)
    )
    attended = (
        (sum_both / mass_both[..., None])
        .reshape(2, TOK_G, heads_dev * head_size)
        .astype(jnp.bfloat16)
    )
    col_width = D // vocab_count
    pair = groups // vocab_count
    head_rows = jnp.transpose(
        out_rows.reshape((vocab_count, pair) + out_weight.shape), (0, 2, 3, 1, 4)
    ).reshape(vocab_count, 2, heads_dev * head_size, col_width)
    column_block = lax.all_to_all(head_rows, "vocab", split_axis=0, concat_axis=0, tiled=True)
    column_block = jnp.transpose(column_block, (1, 0, 2, 3)).reshape(2, D, col_width)
    attended_all = lax.all_gather(attended, "vocab", axis=2, tiled=True)
    mixed_block = jnp.einsum(
        "mtc,mcd->mtd", attended_all, column_block, preferred_element_type=jnp.float32
    )
    mixed = lax.all_gather(mixed_block.astype(jnp.bfloat16), "vocab", axis=2, tiled=True).astype(
        jnp.float32
    )
    hidden_new = (hidden_in.astype(jnp.float32) + rms_scale(mixed, post_gain[:, None, :])).astype(
        jnp.bfloat16
    )
    hidden_out = lax.dynamic_slice_in_dim(hidden_new, vocab_idx * col_width, col_width, 2)
    final = rms_scale(hidden_new.astype(jnp.float32), final_gain[:, None, :]).astype(jnp.bfloat16)
    voc_here = head_weight.shape[2]
    first_column = (group_idx * vocab_count + vocab_idx) * voc_here
    logits = jnp.concatenate(
        [
            jnp.einsum(
                "mtd,mdv->mtv",
                lax.all_gather(final[model : model + 1], "group", axis=1, tiled=True),
                head_weight[model : model + 1],
                preferred_element_type=jnp.float32,
            )
            for model in range(2)
        ]
    )
    highest = jnp.max(logits, axis=-1)
    exp_sum = jnp.sum(jnp.exp(logits - highest[..., None]), axis=-1)
    wanted = targets - first_column
    found = jnp.arange(voc_here, dtype=jnp.int32)[None, :] == wanted[:, None]
    picked = jnp.sum(jnp.where(found[None], logits, 0.0), axis=-1)
    slot_numbers = jnp.arange(request_count, dtype=jnp.int32)
    request_of_slot = jnp.sum(
        jnp.where(owners[None, :] == slot_numbers[:, None], slot_numbers[None, :], 0), axis=1
    )
    place_of_slot = jnp.sum(
        jnp.where(deal[None, :] == request_of_slot[:, None], slot_numbers[None, :], 0), axis=1
    )
    group_of_slot = place_of_slot // SEQ_G
    seq_of_slot = place_of_slot % SEQ_G
    dest_groups = jnp.arange(groups, dtype=jnp.int32)
    slots_per_group = request_count // groups
    row_groups = jnp.concatenate(
        (dest_groups[:, None], group_of_slot.reshape(groups, slots_per_group)), axis=1
    )
    statistics = jnp.stack((highest, exp_sum, picked), axis=0).reshape(3, 2, groups, TOK_G)
    rows = jnp.take(statistics, row_groups.reshape(-1), axis=2).reshape(
        3, 2, groups, 1 + slots_per_group, TOK_G
    )
    rows = jnp.transpose(rows, (2, 3, 0, 1, 4))
    got = lax.all_to_all(rows, "group", split_axis=0, concat_axis=0, tiled=True)
    peak_one = jnp.max(got[:, :, 0], axis=0)
    mass_one = jnp.sum(got[:, :, 1] * jnp.exp(got[:, :, 0] - peak_one[None]), axis=0)
    target_one = jnp.sum(got[:, :, 2], axis=0)
    gathered = lax.all_gather(jnp.stack((peak_one, mass_one, target_one), axis=0), "vocab")
    peak_logit = jnp.max(gathered[:, 0], axis=0)
    exp_total = jnp.sum(gathered[:, 1] * jnp.exp(gathered[:, 0] - peak_logit[None]), axis=0)
    target_logit = jnp.sum(gathered[:, 2], axis=0)
    logprobs = target_logit - (peak_logit + jnp.log(exp_total))
    own_logprobs = logprobs[0]
    my_slots = group_idx * slots_per_group + jnp.arange(slots_per_group, dtype=jnp.int32)
    slot_groups = jnp.take(group_of_slot, my_slots)
    slot_seqs = jnp.take(seq_of_slot, my_slots)
    slot_ids = jnp.take(segment_ids, slot_groups, axis=0)
    in_seq = (slot_ids == slot_seqs[:, None]).astype(jnp.float32)
    slot_gap = logprobs[1:, 0] - logprobs[1:, 1]
    seq_diff = jnp.sum(in_seq * slot_gap, axis=1) / jnp.sum(in_seq, axis=1)
    return (hidden_out, own_logprobs, seq_diff)


def solution(mesh):
    return jax.shard_map(
        shards,
        mesh=mesh,
        in_specs=(
            P(None, "group", None),
            P(None, "group", "vocab"),
            P(None, "vocab", "group"),
            P(None, "vocab"),
            P(None, "vocab"),
            P(),
            P(),
            P(None, None, ("group", "vocab")),
            P(None, "group", None, "vocab"),
            P(None, "group", None, "vocab"),
            P(),
            P(),
            P(),
            P(),
            P(),
            P(),
        ),
        out_specs=(P(None, "group", "vocab"), P(None, "group"), P("group")),
        check_vma=False,
    )
```
